512 devices in a mesh: rows: 64 (over x, z), batch: 8 (over y, core).
Axes of the slice: x: 4, y: 4, z: 16, core: 2. Of those that a mesh axis runs over, the one named last changes fastest.
Arguments:
- frames: bfloat16 [16384, 4096], P('rows', 'batch'), may hold values from -40 to 40
- tap_table: int32 [63], replicated, may hold values from -128 to 127
- sketch_matrix: bfloat16 [512, 256], replicated, may hold values from -0.25 to 0.25
- decay_rates: float32 [8, 256], P('batch'), may hold values from 0.5 to 1
Outputs:
- basis: float32 [8, 16384, 256], P('batch', 'rows')
- factor: float32 [8, 256, 256], P('batch')
- coeffs: float32 [8, 256, 512], P('batch')
The draws below stay inside these ranges and needn't reach their ends.
All inputs are finite; a program needn't handle non-finite values.
Results may differ from the reference program's by a relative error of at most 0.0039.
The reference program's roundings to bfloat16 on the way count: a program that leaves them out, or rounds other values in their place, can miss the bound.
Values may be sent and summed in bfloat16 or wider, within the bound.
No kernel may reach another device: no remote copies, remote signals or barrier semaphores. Data moves between devices by JAX's collectives and lax.ppermute only.
A program may use at most 64 MiB of HBM per device.

```python
import math
import jax
import jax.numpy as jnp
from jax import lax

FR = 512
K = 256
TAPS = 63
NBATCH = 8
NFRAMES = 4096
NPOINTS = 16384


def draw_frames(key, part):
    place = jax.lax.broadcasted_iota(jnp.float32, (NPOINTS, NFRAMES), 0) / NPOINTS
    values = jnp.clip(jax.random.normal(key, (NPOINTS, NFRAMES), jnp.float32), -4.0, 4.0)
    scale = jnp.exp(math.log(4.0) * place)
    return (values * scale).astype(jnp.bfloat16)


def place_ends(entries, key, least, high):
    shape = entries.shape
    spot = [jax.random.randint(jax.random.fold_in(key, axis), (), 0, shape[axis]) for axis in range(len(shape))]
    entries = entries.at[tuple(spot)].set(least)
    longest = shape.index(max(shape))
    spot[longest] = (spot[longest] + 1) % shape[longest]
    return entries.at[tuple(spot)].set(high)


def levels(stream_key, extent, cuts, low, top_value):
    def one(position, shards_of):
        heights = jax.random.uniform(jax.random.fold_in(jax.random.fold_in(stream_key, 6), position), (shards_of,), jnp.float32, low / len(cuts), top_value / len(cuts))
        return jnp.repeat(jnp.exp(heights), extent[position] // shards_of).reshape((-1,) + (1,) * (len(extent) - position - 1))

    gain = one(*cuts[0])
    for cut in cuts[1:]:
        gain = gain * one(*cut)
    return gain


def normal_values(rng, extent, width, most, kind=jnp.bfloat16):
    drawn = width * jax.random.normal(rng, extent, jnp.float32)
    return jnp.clip(drawn, min=-most, max=most).astype(kind)


def setup_inputs(seed: int = 0) -> dict:
    key_list = jax.random.split(jax.random.key(seed), 5)
    frames = draw_frames(jax.random.fold_in(key_list[4], 71), 0)
    tap_table = place_ends(jax.random.randint(key_list[1], (TAPS,), -128, 128), jax.random.fold_in(key_list[1], 1), -128, 127).astype(jnp.int32)
    sketch_matrix = normal_values(key_list[2], (FR, K), FR ** -0.5, 0.25)
    decay_rates = jnp.clip(0.5 + 0.5 * jax.random.uniform(key_list[3], (NBATCH, K), jnp.float32) ** levels(key_list[3], (NBATCH, K), ((0, 8),), -0.2, 0.2), 0.5, 1.0)
    return dict(frames=frames, tap_table=tap_table, sketch_matrix=sketch_matrix, decay_rates=decay_rates)


HIGH = lax.Precision.HIGHEST

def band_matrix(coefs, rows_count, cols_count, offset):
    row_ids = lax.broadcasted_iota(jnp.int32, (rows_count, cols_count), 0)
    col_ids = lax.broadcasted_iota(jnp.int32, (rows_count, cols_count), 1)
    lag_ids = col_ids - row_ids + offset
    valid = (lag_ids >= 0) & (lag_ids < coefs.shape[0])
    values = jnp.take(coefs, jnp.clip(lag_ids, 0, coefs.shape[0] - 1))
    return jnp.where(valid, values, jnp.zeros_like(values))

def gram_of(block):
    return lax.dot_general(block.astype(jnp.float32), block.astype(jnp.float32), (((0,), (0,)), ((), ())), precision=HIGH, preferred_element_type=jnp.float32)

def reference(frames, tap_table, sketch_matrix, decay_rates):
    npoints = frames.shape[0]
    nbatch = decay_rates.shape[0]
    coefs = (tap_table.astype(jnp.float32) / 1024.0).astype(jnp.bfloat16).astype(jnp.float32)
    main_band = band_matrix(coefs, FR, FR, 0)
    hist_band = band_matrix(coefs, TAPS - 1, FR, TAPS - 1)
    blocks = jnp.transpose(frames.reshape(npoints, nbatch, FR), (1, 0, 2))
    histories = jnp.concatenate([jnp.zeros((1, npoints, TAPS - 1), frames.dtype), blocks[:-1, :, FR - (TAPS - 1):]], axis=0)
    sketch_wide = sketch_matrix.astype(jnp.float32)
    root_points = math.sqrt(npoints)

    def section(carried, inputs):
        block, history, rates = inputs
        filtered = (jnp.dot(block.astype(jnp.float32), main_band, precision=HIGH) + jnp.dot(history.astype(jnp.float32), hist_band, precision=HIGH)).astype(jnp.bfloat16)
        sketched = jnp.dot(filtered.astype(jnp.float32), sketch_wide, precision=HIGH)
        weighted = rates[None, :] * carried + sketched
        lower_one = jnp.linalg.cholesky(gram_of(weighted))
        final_q = lax.linalg.triangular_solve(lower_one, weighted, left_side=False, lower=True, transpose_a=True)
        scaled = final_q * root_points
        projected = lax.dot_general(scaled.astype(jnp.float32), filtered.astype(jnp.float32), (((0,), (0,)), ((), ())), precision=HIGH, preferred_element_type=jnp.float32)
        projected = projected * (math.sqrt(K) / npoints)
        return (weighted, (scaled, lower_one.T / root_points, projected))
    start = jnp.zeros((npoints, K), jnp.float32)
    last, outputs = lax.scan(section, start, (blocks, histories, decay_rates))
    return (outputs[0], outputs[1], outputs[2])
```

```python
import math

import jax
import jax.numpy as jnp
from jax import lax
from jax.sharding import Mesh
from jax.sharding import PartitionSpec as P

HIGH = lax.Precision.HIGHEST
ROWS = ("x", "z")
BATCH = ("y", "core")
BLOCK = 128


def shifted(x, axis, by):
    length = lax.axis_size(axis)
    pairs = [(i, i + by) for i in range(length) if 0 <= i + by < length]
    return lax.ppermute(x, axis, pairs)


def band_block(coefs, offset):
    row_ids = lax.broadcasted_iota(jnp.int32, (BLOCK, BLOCK), 0)
    col_ids = lax.broadcasted_iota(jnp.int32, (BLOCK, BLOCK), 1)
    lag_ids = col_ids - row_ids + offset
    block = jnp.zeros((BLOCK, BLOCK), jnp.float32)
    for k in range(coefs.shape[0]):
        block = jnp.where(lag_ids == k, coefs[k], block)
    return block.astype(jnp.bfloat16)


def halve(cur):
    if cur.shape[0] > 8:
        h = cur.shape[0] // 2
        return cur[:h], cur[h:], 0
    h = cur.shape[1] // 2
    return cur[:, :h], cur[:, h:], 1


def reduce_rows(x):
    sizes = {a: lax.axis_size(a) for a in ROWS}
    rounds = []
    d = 1
    while d < max(sizes.values()):
        for a in ROWS:
            if d < sizes[a]:
                rounds.append((a, d))
        d *= 2
    cur = x
    kept = []
    for a, d in rounds:
        bit = (lax.axis_index(a) // d) % 2 == 1
        lo, hi, dim = halve(cur)
        keep = jnp.where(bit, hi, lo)
        send = jnp.where(bit, lo, hi)
        pairs = [(i, i ^ d) for i in range(sizes[a])]
        cur = keep + lax.ppermute(send, a, pairs)
        kept.append(dim)
    for (a, d), dim in zip(reversed(rounds), reversed(kept)):
        bit = (lax.axis_index(a) // d) % 2 == 1
        pairs = [(i, i ^ d) for i in range(sizes[a])]
        other = lax.ppermute(cur, a, pairs)
        cur = jnp.where(
            bit,
            jnp.concatenate([other, cur], axis=dim),
            jnp.concatenate([cur, other], axis=dim),
        )
    return cur


def shards(frames, tap_table, sketch_matrix, decay_rates):
    rows_here, frame_count = frames.shape
    npoints = rows_here * math.prod(lax.axis_size(a) for a in ROWS)
    batch_count = lax.axis_size(BATCH)
    coefs = (tap_table.astype(jnp.float32) / 1024.0).astype(jnp.bfloat16).astype(jnp.float32)
    inner = band_block(coefs, 0)
    carry = band_block(coefs, BLOCK)
    nblocks = frame_count // BLOCK
    zero = jnp.zeros((BLOCK, BLOCK), jnp.bfloat16)
    main_band = jnp.block(
        [[inner if j == i else (carry if j == i + 1 else zero) for j in range(nblocks)] for i in range(nblocks)]
    )
    history = shifted(frames[:, frame_count - BLOCK :], BATCH, 1)
    main = jnp.dot(frames, main_band, preferred_element_type=jnp.float32)
    edge = jnp.dot(history, carry, preferred_element_type=jnp.float32)
    filtered = (main + jnp.pad(edge, ((0, 0), (0, frame_count - BLOCK)))).astype(jnp.bfloat16)
    sketched = jnp.dot(filtered, sketch_matrix, preferred_element_type=jnp.float32)

    weighted = sketched
    factor = decay_rates[0]
    d = 1
    while d < batch_count:
        got_w, got_f = shifted((weighted, factor), BATCH, d)
        weighted = weighted + factor[None, :] * got_w
        factor = factor * got_f
        d *= 2

    root_points = math.sqrt(npoints)
    rank_count = weighted.shape[1]
    both = jnp.concatenate([weighted, filtered.astype(jnp.float32)], axis=1)
    partial = lax.dot_general(
        weighted, both, (((0,), (0,)), ((), ())), precision=HIGH, preferred_element_type=jnp.float32
    )
    summed = reduce_rows(partial)
    gram = summed[:, :rank_count]
    cross = summed[:, rank_count:]
    lower_one = jnp.linalg.cholesky(gram)
    inverse = lax.linalg.triangular_solve(
        lower_one, jnp.eye(rank_count, dtype=jnp.float32), left_side=True, lower=True
    )
    scaled = jnp.dot(weighted, inverse.T, precision=HIGH) * root_points
    projected = jnp.dot(inverse, cross, precision=HIGH) * (math.sqrt(rank_count) / root_points)
    upper = lower_one.T / root_points
    return (scaled[None], upper[None], projected[None])


def solution(mesh):
    rows_n, batch_n = mesh.devices.shape
    along_x = len({d.coords[0] for d in mesh.devices.flat})
    along_y = len({d.coords[1] for d in mesh.devices.flat})
    devices = mesh.devices.reshape(along_x, rows_n // along_x, along_y, batch_n // along_y)
    fine = Mesh(devices, ("x", "z", "y", "core"))
    placed = (P(ROWS, BATCH), P(), P(), P(BATCH, None))
    return jax.shard_map(
        shards,
        mesh=fine,
        in_specs=placed,
        out_specs=(P(BATCH, ROWS, None), P(BATCH, None, None), P(BATCH, None, None)),
        check_vma=False,
    )
```

```python
import math

import jax
import jax.numpy as jnp
from jax import lax
from jax.experimental import pallas as pl
from jax.experimental.pallas import tpu as pltpu
from jax.sharding import Mesh
from jax.sharding import PartitionSpec as P

HIGH = lax.Precision.HIGHEST
ROWS = ("x", "z")
BATCH = ("y", "core")
BLOCK = 128


def shifted(x, axis, by):
    length = lax.axis_size(axis)
    pairs = [(i, i + by) for i in range(length) if 0 <= i + by < length]
    return lax.ppermute(x, axis, pairs)


def band_kernel(coefs_ref, inner_ref, carry_ref):
    row_ids = lax.broadcasted_iota(jnp.int32, (BLOCK, BLOCK), 0)
    col_ids = lax.broadcasted_iota(jnp.int32, (BLOCK, BLOCK), 1)
    lag_ids = col_ids - row_ids
    inner = jnp.zeros((BLOCK, BLOCK), jnp.float32)
    carry = jnp.zeros((BLOCK, BLOCK), jnp.float32)
    for k in range(coefs_ref.shape[0]):
        tap = coefs_ref[k]
        inner = jnp.where(lag_ids == k, tap, inner)
        carry = jnp.where(lag_ids == k - BLOCK, tap, carry)
    inner_ref[...] = inner.astype(inner_ref.dtype)
    carry_ref[...] = carry.astype(carry_ref.dtype)


def band_blocks(coefs):
    block = jax.ShapeDtypeStruct((BLOCK, BLOCK), jnp.bfloat16)
    vmem = pl.BlockSpec(memory_space=pltpu.VMEM)
    return pl.pallas_call(
        band_kernel,
        out_shape=(block, block),
        in_specs=[pl.BlockSpec(memory_space=pltpu.SMEM)],
        out_specs=(vmem, vmem),
    )(coefs)


def scatter_sum(flat, axis):
    count = lax.axis_size(axis)
    got = lax.all_to_all(flat.reshape(count, -1), axis, 0, 0, tiled=True)
    return jnp.sum(got, axis=0)


def gather_back(flat, axis):
    count = lax.axis_size(axis)
    spread = jnp.broadcast_to(flat[None], (count,) + flat.shape)
    return lax.all_to_all(spread, axis, 0, 0, tiled=True).reshape(-1)


def reduce_rows(x):
    flat = x.reshape(-1)
    flat = scatter_sum(flat, "x")
    flat = scatter_sum(flat, "z")
    flat = gather_back(flat, "z")
    flat = gather_back(flat, "x")
    return flat.reshape(x.shape)


def shards(frames, tap_table, sketch_matrix, decay_rates):
    rows_here, frame_count = frames.shape
    npoints = rows_here * math.prod(lax.axis_size(a) for a in ROWS)
    batch_count = lax.axis_size(BATCH)
    coefs = (tap_table.astype(jnp.float32) / 1024.0).astype(jnp.bfloat16).astype(jnp.float32)
    inner, carry = band_blocks(coefs)
    nblocks = frame_count // BLOCK
    zero = jnp.zeros((BLOCK, BLOCK), jnp.bfloat16)
    main_band = jnp.block(
        [[inner if j == i else (carry if j == i + 1 else zero) for j in range(nblocks)] for i in range(nblocks)]
    )
    history = shifted(frames[:, frame_count - BLOCK :], BATCH, 1)
    main = jnp.dot(frames, main_band, preferred_element_type=jnp.float32)
    edge = jnp.dot(history, carry, preferred_element_type=jnp.float32)
    filtered = (main + jnp.pad(edge, ((0, 0), (0, frame_count - BLOCK)))).astype(jnp.bfloat16)
    sketched = jnp.dot(filtered, sketch_matrix, preferred_element_type=jnp.float32)

    weighted = sketched
    factor = decay_rates[0]
    d = 1
    while d < batch_count:
        got_w, got_f = shifted((weighted, factor), BATCH, d)
        weighted = weighted + factor[None, :] * got_w
        factor = factor * got_f
        d *= 2

    root_points = math.sqrt(npoints)
    rank_count = weighted.shape[1]
    both = jnp.concatenate([weighted, filtered.astype(jnp.float32)], axis=1)
    partial = lax.dot_general(
        weighted, both, (((0,), (0,)), ((), ())), precision=HIGH, preferred_element_type=jnp.float32
    )
    summed = reduce_rows(partial)
    gram = summed[:, :rank_count]
    cross = summed[:, rank_count:]
    lower_one = jnp.linalg.cholesky(gram)
    inverse = lax.linalg.triangular_solve(
        lower_one, jnp.eye(rank_count, dtype=jnp.float32), left_side=True, lower=True
    )
    scaled = jnp.dot(weighted, inverse.T, precision=HIGH) * root_points
    projected = jnp.dot(inverse, cross, precision=HIGH) * (math.sqrt(rank_count) / root_points)
    upper = lower_one.T / root_points
    return (scaled[None], upper[None], projected[None])


def solution(mesh):
    rows_n, batch_n = mesh.devices.shape
    along_x = len({d.coords[0] for d in mesh.devices.flat})
    along_y = len({d.coords[1] for d in mesh.devices.flat})
    devices = mesh.devices.reshape(along_x, rows_n // along_x, along_y, batch_n // along_y)
    fine = Mesh(devices, ("x", "z", "y", "core"))
    placed = (P(ROWS, BATCH), P(), P(), P(BATCH, None))
    return jax.shard_map(
        shards,
        mesh=fine,
        in_specs=placed,
        out_specs=(P(BATCH, ROWS, None), P(BATCH, None, None), P(BATCH, None, None)),
        check_vma=False,
    )
```

```python
import math

import jax
import jax.numpy as jnp
from jax import lax
from jax.experimental import pallas as pl
from jax.experimental.pallas import tpu as pltpu
from jax.sharding import Mesh
from jax.sharding import PartitionSpec as P

HIGH = lax.Precision.HIGHEST
ROWS = ("x", "z")
BATCH = ("y", "core")
BLOCK = 128


def shifted(x, axis, by):
    length = lax.axis_size(axis)
    pairs = [(i, i + by) for i in range(length) if 0 <= i + by < length]
    return lax.ppermute(x, axis, pairs)


def band_kernel(coefs_ref, inner_ref, carry_ref):
    row_ids = lax.broadcasted_iota(jnp.int32, (BLOCK, BLOCK), 0)
    col_ids = lax.broadcasted_iota(jnp.int32, (BLOCK, BLOCK), 1)
    lag_ids = col_ids - row_ids
    inner = jnp.zeros((BLOCK, BLOCK), jnp.float32)
    carry = jnp.zeros((BLOCK, BLOCK), jnp.float32)
    for k in range(coefs_ref.shape[0]):
        tap = coefs_ref[k]
        inner = jnp.where(lag_ids == k, tap, inner)
        carry = jnp.where(lag_ids == k - BLOCK, tap, carry)
    inner_ref[...] = inner.astype(inner_ref.dtype)
    carry_ref[...] = carry.astype(carry_ref.dtype)


def band_blocks(coefs):
    block = jax.ShapeDtypeStruct((BLOCK, BLOCK), jnp.bfloat16)
    vmem = pl.BlockSpec(memory_space=pltpu.VMEM)
    return pl.pallas_call(
        band_kernel,
        out_shape=(block, block),
        in_specs=[pl.BlockSpec(memory_space=pltpu.SMEM)],
        out_specs=(vmem, vmem),
    )(coefs)


def scatter_sum(flat, axis):
    count = lax.axis_size(axis)
    got = lax.all_to_all(flat.reshape(count, -1), axis, 0, 0, tiled=True)
    return jnp.sum(got, axis=0)


def gather_back(flat, axis):
    count = lax.axis_size(axis)
    spread = jnp.broadcast_to(flat[None], (count,) + flat.shape)
    return lax.all_to_all(spread, axis, 0, 0, tiled=True).reshape(-1)


def reduce_rows(x):
    flat = x.reshape(-1)
    flat = scatter_sum(flat, "x")
    flat = scatter_sum(flat, "z")
    flat = gather_back(flat, "z")
    flat = gather_back(flat, "x")
    return flat.reshape(x.shape)


def shards(frames, tap_table, sketch_matrix, decay_rates):
    rows_here, frame_count = frames.shape
    npoints = rows_here * math.prod(lax.axis_size(a) for a in ROWS)
    batch_count = lax.axis_size(BATCH)
    coefs = (tap_table.astype(jnp.float32) / 1024.0).astype(jnp.bfloat16).astype(jnp.float32)
    inner, carry = band_blocks(coefs)
    nblocks = frame_count // BLOCK
    zero = jnp.zeros((BLOCK, BLOCK), jnp.bfloat16)
    main_band = jnp.block(
        [[inner if j == i else (carry if j == i + 1 else zero) for j in range(nblocks)] for i in range(nblocks)]
    )
    history = shifted(frames[:, frame_count - BLOCK :], BATCH, 1)
    main = jnp.dot(frames, main_band, preferred_element_type=jnp.float32)
    edge = jnp.dot(history, carry, preferred_element_type=jnp.float32)
    filtered = (main + jnp.pad(edge, ((0, 0), (0, frame_count - BLOCK)))).astype(jnp.bfloat16)
    sketched = jnp.dot(filtered, sketch_matrix, preferred_element_type=jnp.float32)

    weighted = sketched
    factor = decay_rates[0]
    d = 1
    while d < batch_count:
        got_w, got_f = shifted((weighted, factor), BATCH, d)
        weighted = weighted + factor[None, :] * got_w
        factor = factor * got_f
        d *= 2

    root_points = math.sqrt(npoints)
    rank_count = weighted.shape[1]
    gram = reduce_rows(
        lax.dot_general(
            weighted, weighted, (((0,), (0,)), ((), ())), precision=HIGH, preferred_element_type=jnp.float32
        )
    )
    cross = reduce_rows(
        lax.dot_general(
            weighted,
            filtered.astype(jnp.float32),
            (((0,), (0,)), ((), ())),
            precision=HIGH,
            preferred_element_type=jnp.float32,
        )
    )
    lower_one = jnp.linalg.cholesky(gram)
    inverse = lax.linalg.triangular_solve(
        lower_one, jnp.eye(rank_count, dtype=jnp.float32), left_side=True, lower=True
    )
    scaled = jnp.dot(weighted, inverse.T, precision=HIGH) * root_points
    projected = jnp.dot(inverse, cross, precision=HIGH) * (math.sqrt(rank_count) / root_points)
    upper = lower_one.T / root_points
    return (scaled[None], upper[None], projected[None])


def solution(mesh):
    rows_n, batch_n = mesh.devices.shape
    along_x = len({d.coords[0] for d in mesh.devices.flat})
    along_y = len({d.coords[1] for d in mesh.devices.flat})
    devices = mesh.devices.reshape(along_x, rows_n // along_x, along_y, batch_n // along_y)
    fine = Mesh(devices, ("x", "z", "y", "core"))
    placed = (P(ROWS, BATCH), P(), P(), P(BATCH, None))
    return jax.shard_map(
        shards,
        mesh=fine,
        in_specs=placed,
        out_specs=(P(BATCH, ROWS, None), P(BATCH, None, None), P(BATCH, None, None)),
        check_vma=False,
    )
```

```python
import math

import jax
import jax.numpy as jnp
from jax import lax
from jax.experimental import pallas as pl
from jax.experimental.pallas import tpu as pltpu
from jax.sharding import Mesh
from jax.sharding import PartitionSpec as P

HIGH = lax.Precision.HIGHEST
ROWS = ("x", "z")
BATCH = ("y", "core")
BLOCK = 128


def shifted(x, axis, by):
    length = lax.axis_size(axis)
    pairs = [(i, i + by) for i in range(length) if 0 <= i + by < length]
    return lax.ppermute(x, axis, pairs)


def band_kernel(coefs_ref, inner_ref, carry_ref):
    row_ids = lax.broadcasted_iota(jnp.int32, (BLOCK, BLOCK), 0)
    col_ids = lax.broadcasted_iota(jnp.int32, (BLOCK, BLOCK), 1)
    lag_ids = col_ids - row_ids
    inner = jnp.zeros((BLOCK, BLOCK), jnp.float32)
    carry = jnp.zeros((BLOCK, BLOCK), jnp.float32)
    for k in range(coefs_ref.shape[0]):
        tap = coefs_ref[k]
        inner = jnp.where(lag_ids == k, tap, inner)
        carry = jnp.where(lag_ids == k - BLOCK, tap, carry)
    inner_ref[...] = inner.astype(inner_ref.dtype)
    carry_ref[...] = carry.astype(carry_ref.dtype)


def band_blocks(coefs):
    block = jax.ShapeDtypeStruct((BLOCK, BLOCK), jnp.bfloat16)
    vmem = pl.BlockSpec(memory_space=pltpu.VMEM)
    return pl.pallas_call(
        band_kernel,
        out_shape=(block, block),
        in_specs=[pl.BlockSpec(memory_space=pltpu.SMEM)],
        out_specs=(vmem, vmem),
    )(coefs)


def scatter_sum(flat, axis):
    count = lax.axis_size(axis)
    got = lax.all_to_all(flat.reshape(count, -1), axis, 0, 0, tiled=True)
    return jnp.sum(got, axis=0)


def gather_back(flat, axis):
    count = lax.axis_size(axis)
    spread = jnp.broadcast_to(flat[None], (count,) + flat.shape)
    return lax.all_to_all(spread, axis, 0, 0, tiled=True).reshape(-1)


def reduce_rows(x):
    flat = x.reshape(-1)
    flat = scatter_sum(flat, "x")
    flat = scatter_sum(flat, "z")
    flat = gather_back(flat, "z")
    flat = gather_back(flat, "x")
    return flat.reshape(x.shape)


def factor_and_invert(gram):
    h = gram.shape[0] // 2
    eye = jnp.eye(h, dtype=jnp.float32)
    l11 = lax.linalg.cholesky(gram[:h, :h])
    i11 = lax.linalg.triangular_solve(l11, eye, left_side=True, lower=True)
    l21 = jnp.dot(gram[h:, :h], i11.T, precision=HIGH)
    l22 = lax.linalg.cholesky(gram[h:, h:] - jnp.dot(l21, l21.T, precision=HIGH))
    i22 = lax.linalg.triangular_solve(l22, eye, left_side=True, lower=True)
    x21 = -jnp.dot(i22, jnp.dot(l21, i11, precision=HIGH), precision=HIGH)
    zero = jnp.zeros((h, h), jnp.float32)
    return jnp.block([[l11, zero], [l21, l22]]), jnp.block([[i11, zero], [x21, i22]])


def shards(frames, tap_table, sketch_matrix, decay_rates):
    rows_here, frame_count = frames.shape
    npoints = rows_here * math.prod(lax.axis_size(a) for a in ROWS)
    batch_count = lax.axis_size(BATCH)
    coefs = (tap_table.astype(jnp.float32) / 1024.0).astype(jnp.bfloat16).astype(jnp.float32)
    inner, carry = band_blocks(coefs)
    nblocks = frame_count // BLOCK
    zero = jnp.zeros((BLOCK, BLOCK), jnp.bfloat16)
    main_band = jnp.block(
        [[inner if j == i else (carry if j == i + 1 else zero) for j in range(nblocks)] for i in range(nblocks)]
    )
    history = shifted(frames[:, frame_count - BLOCK :], BATCH, 1)
    main = jnp.dot(frames, main_band, preferred_element_type=jnp.float32)
    edge = jnp.dot(history, carry, preferred_element_type=jnp.float32)
    filtered = (main + jnp.pad(edge, ((0, 0), (0, frame_count - BLOCK)))).astype(jnp.bfloat16)
    sketched = jnp.dot(filtered, sketch_matrix, preferred_element_type=jnp.float32)

    factors = []
    factor = decay_rates[0]
    d = 1
    while d < batch_count:
        factors.append(factor)
        factor = factor * shifted(factor, BATCH, d)
        d *= 2
    weighted = sketched
    d = 1
    for factor in factors:
        weighted = weighted + factor[None, :] * shifted(weighted, BATCH, d)
        d *= 2

    root_points = math.sqrt(npoints)
    rank_count = weighted.shape[1]
    both = jnp.concatenate([weighted, filtered.astype(jnp.float32)], axis=1)
    partial = lax.dot_general(
        weighted, both, (((0,), (0,)), ((), ())), precision=HIGH, preferred_element_type=jnp.float32
    )
    summed = reduce_rows(partial)
    gram = summed[:, :rank_count]
    cross = summed[:, rank_count:]
    lower_one, inverse = factor_and_invert(gram)
    scaled = jnp.dot(weighted, inverse.T, precision=HIGH) * root_points
    projected = jnp.dot(inverse, cross, precision=HIGH) * (math.sqrt(rank_count) / root_points)
    upper = lower_one.T / root_points
    return (scaled[None], upper[None], projected[None])


def solution(mesh):
    rows_n, batch_n = mesh.devices.shape
    along_x = len({d.coords[0] for d in mesh.devices.flat})
    along_y = len({d.coords[1] for d in mesh.devices.flat})
    devices = mesh.devices.reshape(along_x, rows_n // along_x, along_y, batch_n // along_y)
    fine = Mesh(devices, ("x", "z", "y", "core"))
    placed = (P(ROWS, BATCH), P(), P(), P(BATCH, None))
    return jax.shard_map(
        shards,
        mesh=fine,
        in_specs=placed,
        out_specs=(P(BATCH, ROWS, None), P(BATCH, None, None), P(BATCH, None, None)),
        check_vma=False,
    )
```

```python
import math

import jax
import jax.numpy as jnp
from jax import lax
from jax.experimental import pallas as pl
from jax.experimental.pallas import tpu as pltpu
from jax.sharding import Mesh
from jax.sharding import PartitionSpec as P

HIGH = lax.Precision.HIGHEST
ROWS = ("x", "z")
BATCH = ("y", "core")
BLOCK = 128


def shifted(x, axis, by):
    length = lax.axis_size(axis)
    pairs = [(i, i + by) for i in range(length) if 0 <= i + by < length]
    return lax.ppermute(x, axis, pairs)


def band_kernel(coefs_ref, inner_ref, carry_ref):
    row_ids = lax.broadcasted_iota(jnp.int32, (BLOCK, BLOCK), 0)
    col_ids = lax.broadcasted_iota(jnp.int32, (BLOCK, BLOCK), 1)
    lag_ids = col_ids - row_ids
    inner = jnp.zeros((BLOCK, BLOCK), jnp.float32)
    carry = jnp.zeros((BLOCK, BLOCK), jnp.float32)
    for k in range(coefs_ref.shape[0]):
        tap = coefs_ref[k]
        inner = jnp.where(lag_ids == k, tap, inner)
        carry = jnp.where(lag_ids == k - BLOCK, tap, carry)
    inner_ref[...] = inner.astype(inner_ref.dtype)
    carry_ref[...] = carry.astype(carry_ref.dtype)


def band_blocks(coefs):
    block = jax.ShapeDtypeStruct((BLOCK, BLOCK), jnp.bfloat16)
    vmem = pl.BlockSpec(memory_space=pltpu.VMEM)
    return pl.pallas_call(
        band_kernel,
        out_shape=(block, block),
        in_specs=[pl.BlockSpec(memory_space=pltpu.SMEM)],
        out_specs=(vmem, vmem),
    )(coefs)


def scatter_sum(flat, axis):
    count = lax.axis_size(axis)
    got = lax.all_to_all(flat.reshape(count, -1), axis, 0, 0, tiled=True)
    return jnp.sum(got, axis=0)


def gather_back(flat, axis):
    count = lax.axis_size(axis)
    spread = jnp.broadcast_to(flat[None], (count,) + flat.shape)
    return lax.all_to_all(spread, axis, 0, 0, tiled=True).reshape(-1)


def reduce_rows(x):
    flat = x.reshape(-1)
    flat = scatter_sum(flat, "x")
    flat = scatter_sum(flat, "z")
    flat = gather_back(flat, "z")
    flat = gather_back(flat, "x")
    return flat.reshape(x.shape)


def factor_and_invert(gram):
    h = gram.shape[0] // 2
    eye = jnp.eye(h, dtype=jnp.float32)
    l11 = lax.linalg.cholesky(gram[:h, :h])
    i11 = lax.linalg.triangular_solve(l11, eye, left_side=True, lower=True)
    l21 = jnp.dot(gram[h:, :h], i11.T, precision=HIGH)
    l22 = lax.linalg.cholesky(gram[h:, h:] - jnp.dot(l21, l21.T, precision=HIGH))
    i22 = lax.linalg.triangular_solve(l22, eye, left_side=True, lower=True)
    x21 = -jnp.dot(i22, jnp.dot(l21, i11, precision=HIGH), precision=HIGH)
    zero = jnp.zeros((h, h), jnp.float32)
    return jnp.block([[l11, zero], [l21, l22]]), jnp.block([[i11, zero], [x21, i22]])


def shards(frames, tap_table, sketch_matrix, decay_rates):
    rows_here, frame_count = frames.shape
    npoints = rows_here * math.prod(lax.axis_size(a) for a in ROWS)
    batch_count = lax.axis_size(BATCH)
    coefs = (tap_table.astype(jnp.float32) / 1024.0).astype(jnp.bfloat16).astype(jnp.float32)
    inner, carry = band_blocks(coefs)
    nblocks = frame_count // BLOCK
    zero = jnp.zeros((BLOCK, BLOCK), jnp.bfloat16)
    main_band = jnp.block(
        [[inner if j == i else (carry if j == i + 1 else zero) for j in range(nblocks)] for i in range(nblocks)]
    )
    history = shifted(frames[:, frame_count - BLOCK :], BATCH, 1)
    main = jnp.dot(frames, main_band, preferred_element_type=jnp.float32)
    edge = jnp.dot(history, carry, preferred_element_type=jnp.float32)
    filtered = (main + jnp.pad(edge, ((0, 0), (0, frame_count - BLOCK)))).astype(jnp.bfloat16)
    sketched = jnp.dot(filtered, sketch_matrix, preferred_element_type=jnp.float32)

    weighted = sketched
    factor = jnp.broadcast_to(decay_rates[0][None, :], (8, weighted.shape[1]))
    d = 1
    while d < batch_count:
        if 2 * d < batch_count:
            got = shifted(jnp.concatenate([weighted, factor], axis=0), BATCH, d)
            got_w, got_f = got[: weighted.shape[0]], got[weighted.shape[0] :]
        else:
            got_w, got_f = shifted(weighted, BATCH, d), None
        weighted = weighted + factor[:1] * got_w
        if got_f is not None:
            factor = factor * got_f
        d *= 2

    root_points = math.sqrt(npoints)
    rank_count = weighted.shape[1]
    both = jnp.concatenate([weighted, filtered.astype(jnp.float32)], axis=1)
    partial = lax.dot_general(
        weighted, both, (((0,), (0,)), ((), ())), precision=HIGH, preferred_element_type=jnp.float32
    )
    summed = reduce_rows(partial)
    gram = summed[:, :rank_count]
    cross = summed[:, rank_count:]
    lower_one, inverse = factor_and_invert(gram)
    scaled = jnp.dot(weighted, inverse.T, precision=HIGH) * root_points
    projected = jnp.dot(inverse, cross, precision=HIGH) * (math.sqrt(rank_count) / root_points)
    upper = lower_one.T / root_points
    return (scaled[None], upper[None], projected[None])


def solution(mesh):
    rows_n, batch_n = mesh.devices.shape
    along_x = len({d.coords[0] for d in mesh.devices.flat})
    along_y = len({d.coords[1] for d in mesh.devices.flat})
    devices = mesh.devices.reshape(along_x, rows_n // along_x, along_y, batch_n // along_y)
    fine = Mesh(devices, ("x", "z", "y", "core"))
    placed = (P(ROWS, BATCH), P(), P(), P(BATCH, None))
    return jax.shard_map(
        shards,
        mesh=fine,
        in_specs=placed,
        out_specs=(P(BATCH, ROWS, None), P(BATCH, None, None), P(BATCH, None, None)),
        check_vma=False,
    )
```

```python
import math

import jax
import jax.numpy as jnp
from jax import lax
from jax.experimental import pallas as pl
from jax.experimental.pallas import tpu as pltpu
from jax.sharding import Mesh
from jax.sharding import PartitionSpec as P

HIGH = lax.Precision.HIGHEST
ROWS = ("x", "z")
BATCH = ("y", "core")
BLOCK = 128


def shifted(x, axis, by):
    length = lax.axis_size(axis)
    pairs = [(i, i + by) for i in range(length) if 0 <= i + by < length]
    return lax.ppermute(x, axis, pairs)


def band_kernel(coefs_ref, inner_ref, carry_ref):
    row_ids = lax.broadcasted_iota(jnp.int32, (BLOCK, BLOCK), 0)
    col_ids = lax.broadcasted_iota(jnp.int32, (BLOCK, BLOCK), 1)
    lag_ids = col_ids - row_ids
    inner = jnp.zeros((BLOCK, BLOCK), jnp.float32)
    carry = jnp.zeros((BLOCK, BLOCK), jnp.float32)
    for k in range(coefs_ref.shape[0]):
        tap = coefs_ref[k]
        inner = jnp.where(lag_ids == k, tap, inner)
        carry = jnp.where(lag_ids == k - BLOCK, tap, carry)
    inner_ref[...] = inner.astype(inner_ref.dtype)
    carry_ref[...] = carry.astype(carry_ref.dtype)


def band_blocks(coefs):
    block = jax.ShapeDtypeStruct((BLOCK, BLOCK), jnp.bfloat16)
    vmem = pl.BlockSpec(memory_space=pltpu.VMEM)
    return pl.pallas_call(
        band_kernel,
        out_shape=(block, block),
        in_specs=[pl.BlockSpec(memory_space=pltpu.SMEM)],
        out_specs=(vmem, vmem),
    )(coefs)


def scatter_sum(flat, axis):
    count = lax.axis_size(axis)
    got = lax.all_to_all(flat.reshape(count, -1), axis, 0, 0, tiled=True)
    return jnp.sum(got, axis=0)


def gather_back(flat, axis):
    count = lax.axis_size(axis)
    spread = jnp.broadcast_to(flat[None], (count,) + flat.shape)
    return lax.all_to_all(spread, axis, 0, 0, tiled=True).reshape(-1)


def reduce_rows(x):
    flat = x.reshape(-1)
    flat = scatter_sum(flat, "x")
    flat = scatter_sum(flat, "z")
    flat = gather_back(flat, "z")
    flat = gather_back(flat, "x")
    return flat.reshape(x.shape)


def chol_kernel(g_ref, out_ref, a_ref):
    n = g_ref.shape[0]
    rows = lax.broadcasted_iota(jnp.int32, (n, n), 0)
    cols = lax.broadcasted_iota(jnp.int32, (n, n), 1)
    a_ref[:, :n] = g_ref[...]
    a_ref[:, n:] = jnp.where(rows == cols, 1.0, 0.0).astype(jnp.float32)
    sub = lax.broadcasted_iota(jnp.int32, (n, 2 * n), 0)
    lane = lax.broadcasted_iota(jnp.int32, (n, 2 * n), 1)
    lane_row = lax.broadcasted_iota(jnp.int32, (1, 2 * n), 1)

    def step(j, carry):
        row = a_ref[pl.ds(j, 1), :]
        pivot = jnp.sum(jnp.where(lane_row == j, row, 0.0), axis=1, keepdims=True)
        scale = 1.0 / jnp.sqrt(pivot)
        top = jnp.where(lane_row >= j, row * scale, 0.0)
        whole = a_ref[...]
        column = jnp.sum(jnp.where(lane == j, whole, 0.0), axis=1, keepdims=True) * scale
        a_ref[...] = jnp.where(sub > j, whole - column * top, jnp.where(sub == j, top, whole))
        return carry

    lax.fori_loop(0, n, step, 0)
    out_ref[...] = a_ref[...]

def factor_block(g):
    n = g.shape[0]
    vmem = pl.BlockSpec(memory_space=pltpu.VMEM)
    out = pl.pallas_call(chol_kernel, out_shape=jax.ShapeDtypeStruct((n, 2 * n), jnp.float32),
        in_specs=[vmem], out_specs=vmem, scratch_shapes=[pltpu.VMEM((n, 2 * n), jnp.float32)])(g)
    return out[:, :n].T, out[:, n:]


def factor_and_invert(gram):
    h = gram.shape[0] // 2
    l11, i11 = factor_block(gram[:h, :h])
    l21 = jnp.dot(gram[h:, :h], i11.T, precision=HIGH)
    l22, i22 = factor_block(gram[h:, h:] - jnp.dot(l21, l21.T, precision=HIGH))
    x21 = -jnp.dot(i22, jnp.dot(l21, i11, precision=HIGH), precision=HIGH)
    zero = jnp.zeros((h, h), jnp.float32)
    return jnp.block([[l11, zero], [l21, l22]]), jnp.block([[i11, zero], [x21, i22]])


def shards(frames, tap_table, sketch_matrix, decay_rates):
    rows_here, frame_count = frames.shape
    npoints = rows_here * math.prod(lax.axis_size(a) for a in ROWS)
    batch_count = lax.axis_size(BATCH)
    coefs = (tap_table.astype(jnp.float32) / 1024.0).astype(jnp.bfloat16).astype(jnp.float32)
    inner, carry = band_blocks(coefs)
    nblocks = frame_count // BLOCK
    zero = jnp.zeros((BLOCK, BLOCK), jnp.bfloat16)
    main_band = jnp.block(
        [[inner if j == i else (carry if j == i + 1 else zero) for j in range(nblocks)] for i in range(nblocks)]
    )
    history = shifted(frames[:, frame_count - BLOCK :], BATCH, 1)
    main = jnp.dot(frames, main_band, preferred_element_type=jnp.float32)
    edge = jnp.dot(history, carry, preferred_element_type=jnp.float32)
    filtered = (main + jnp.pad(edge, ((0, 0), (0, frame_count - BLOCK)))).astype(jnp.bfloat16)
    sketched = jnp.dot(filtered, sketch_matrix, preferred_element_type=jnp.float32)

    factors = []
    factor = decay_rates[0]
    d = 1
    while d < batch_count:
        factors.append(factor)
        factor = factor * shifted(factor, BATCH, d)
        d *= 2
    weighted = sketched
    d = 1
    for factor in factors:
        weighted = weighted + factor[None, :] * shifted(weighted, BATCH, d)
        d *= 2

    root_points = math.sqrt(npoints)
    rank_count = weighted.shape[1]
    both = jnp.concatenate([weighted, filtered.astype(jnp.float32)], axis=1)
    partial = lax.dot_general(
        weighted, both, (((0,), (0,)), ((), ())), precision=HIGH, preferred_element_type=jnp.float32
    )
    summed = reduce_rows(partial)
    gram = summed[:, :rank_count]
    cross = summed[:, rank_count:]
    lower_one, inverse = factor_and_invert(gram)
    scaled = jnp.dot(weighted, inverse.T, precision=HIGH) * root_points
    projected = jnp.dot(inverse, cross, precision=HIGH) * (math.sqrt(rank_count) / root_points)
    upper = lower_one.T / root_points
    return (scaled[None], upper[None], projected[None])


def solution(mesh):
    rows_n, batch_n = mesh.devices.shape
    along_x = len({d.coords[0] for d in mesh.devices.flat})
    along_y = len({d.coords[1] for d in mesh.devices.flat})
    devices = mesh.devices.reshape(along_x, rows_n // along_x, along_y, batch_n // along_y)
    fine = Mesh(devices, ("x", "z", "y", "core"))
    placed = (P(ROWS, BATCH), P(), P(), P(BATCH, None))
    return jax.shard_map(
        shards,
        mesh=fine,
        in_specs=placed,
        out_specs=(P(BATCH, ROWS, None), P(BATCH, None, None), P(BATCH, None, None)),
        check_vma=False,
    )
```

```python
import math

import jax
import jax.numpy as jnp
from jax import lax
from jax.experimental import pallas as pl
from jax.experimental.pallas import tpu as pltpu
from jax.sharding import Mesh
from jax.sharding import PartitionSpec as P

HIGH = lax.Precision.HIGHEST
ROWS = ("x", "z")
BATCH = ("y", "core")
BLOCK = 128


def shifted(x, axis, by):
    length = lax.axis_size(axis)
    pairs = [(i, i + by) for i in range(length) if 0 <= i + by < length]
    return lax.ppermute(x, axis, pairs)


def band_kernel(coefs_ref, inner_ref, carry_ref):
    row_ids = lax.broadcasted_iota(jnp.int32, (BLOCK, BLOCK), 0)
    col_ids = lax.broadcasted_iota(jnp.int32, (BLOCK, BLOCK), 1)
    lag_ids = col_ids - row_ids
    inner = jnp.zeros((BLOCK, BLOCK), jnp.float32)
    carry = jnp.zeros((BLOCK, BLOCK), jnp.float32)
    for k in range(coefs_ref.shape[0]):
        tap = coefs_ref[k]
        inner = jnp.where(lag_ids == k, tap, inner)
        carry = jnp.where(lag_ids == k - BLOCK, tap, carry)
    inner_ref[...] = inner.astype(inner_ref.dtype)
    carry_ref[...] = carry.astype(carry_ref.dtype)


def band_blocks(coefs):
    block = jax.ShapeDtypeStruct((BLOCK, BLOCK), jnp.bfloat16)
    vmem = pl.BlockSpec(memory_space=pltpu.VMEM)
    return pl.pallas_call(
        band_kernel,
        out_shape=(block, block),
        in_specs=[pl.BlockSpec(memory_space=pltpu.SMEM)],
        out_specs=(vmem, vmem),
    )(coefs)


def scatter_sum(flat, axis):
    count = lax.axis_size(axis)
    got = lax.all_to_all(flat.reshape(count, -1), axis, 0, 0, tiled=True)
    return jnp.sum(got, axis=0)


def gather_back(flat, axis):
    count = lax.axis_size(axis)
    spread = jnp.broadcast_to(flat[None], (count,) + flat.shape)
    return lax.all_to_all(spread, axis, 0, 0, tiled=True).reshape(-1)


def reduce_rows(x):
    flat = x.reshape(-1)
    flat = scatter_sum(flat, "x")
    flat = scatter_sum(flat, "z")
    flat = gather_back(flat, "z")
    flat = gather_back(flat, "x")
    return flat.reshape(x.shape)


def chol_kernel(g_ref, out_ref, a_ref):
    n = g_ref.shape[0]
    rows = lax.broadcasted_iota(jnp.int32, (n, n), 0)
    cols = lax.broadcasted_iota(jnp.int32, (n, n), 1)
    a_ref[:, :n] = g_ref[...]
    a_ref[:, n:] = jnp.where(rows == cols, 1.0, 0.0).astype(jnp.float32)
    lane_row = lax.broadcasted_iota(jnp.int32, (1, 2 * n), 1)
    for lo in range(0, n, 8):
        count = n - lo
        sub = lax.broadcasted_iota(jnp.int32, (count, 2 * n), 0) + lo
        lane = lax.broadcasted_iota(jnp.int32, (count, n), 1)

        def step(j, carry, lo=lo, sub=sub, lane=lane):
            row = a_ref[pl.ds(j, 1), :]
            pivot = jnp.sum(jnp.where(lane_row == j, row, 0.0), axis=1, keepdims=True)
            scale = 1.0 / jnp.sqrt(pivot)
            top = jnp.where(lane_row >= j, row * scale, 0.0)
            whole = a_ref[lo:, :]
            column = jnp.sum(jnp.where(lane == j, whole[:, :n], 0.0), axis=1, keepdims=True) * scale
            a_ref[lo:, :] = jnp.where(sub > j, whole - column * top, jnp.where(sub == j, top, whole))
            return carry

        lax.fori_loop(lo, lo + 8, step, 0, unroll=True)
    out_ref[...] = a_ref[...]


def factor_block(g):
    n = g.shape[0]
    vmem = pl.BlockSpec(memory_space=pltpu.VMEM)
    out = pl.pallas_call(chol_kernel, out_shape=jax.ShapeDtypeStruct((n, 2 * n), jnp.float32),
        in_specs=[vmem], out_specs=vmem, scratch_shapes=[pltpu.VMEM((n, 2 * n), jnp.float32)])(g)
    return out[:, :n].T, out[:, n:]


def factor_and_invert(gram):
    h = gram.shape[0] // 2
    l11, i11 = factor_block(gram[:h, :h])
    l21 = jnp.dot(gram[h:, :h], i11.T, precision=HIGH)
    l22, i22 = factor_block(gram[h:, h:] - jnp.dot(l21, l21.T, precision=HIGH))
    x21 = -jnp.dot(i22, jnp.dot(l21, i11, precision=HIGH), precision=HIGH)
    zero = jnp.zeros((h, h), jnp.float32)
    return jnp.block([[l11, zero], [l21, l22]]), jnp.block([[i11, zero], [x21, i22]])


def shards(frames, tap_table, sketch_matrix, decay_rates):
    rows_here, frame_count = frames.shape
    npoints = rows_here * math.prod(lax.axis_size(a) for a in ROWS)
    batch_count = lax.axis_size(BATCH)
    coefs = (tap_table.astype(jnp.float32) / 1024.0).astype(jnp.bfloat16).astype(jnp.float32)
    inner, carry = band_blocks(coefs)
    nblocks = frame_count // BLOCK
    zero = jnp.zeros((BLOCK, BLOCK), jnp.bfloat16)
    main_band = jnp.block(
        [[inner if j == i else (carry if j == i + 1 else zero) for j in range(nblocks)] for i in range(nblocks)]
    )
    history = shifted(frames[:, frame_count - BLOCK :], BATCH, 1)
    main = jnp.dot(frames, main_band, preferred_element_type=jnp.float32)
    edge = jnp.dot(history, carry, preferred_element_type=jnp.float32)
    filtered = (main + jnp.pad(edge, ((0, 0), (0, frame_count - BLOCK)))).astype(jnp.bfloat16)
    sketched = jnp.dot(filtered, sketch_matrix, preferred_element_type=jnp.float32)

    factors = []
    factor = decay_rates[0]
    d = 1
    while d < batch_count:
        factors.append(factor)
        factor = factor * shifted(factor, BATCH, d)
        d *= 2
    weighted = sketched
    d = 1
    for factor in factors:
        weighted = weighted + factor[None, :] * shifted(weighted, BATCH, d)
        d *= 2

    root_points = math.sqrt(npoints)
    rank_count = weighted.shape[1]
    both = jnp.concatenate([weighted, filtered.astype(jnp.float32)], axis=1)
    partial = lax.dot_general(
        weighted, both, (((0,), (0,)), ((), ())), precision=HIGH, preferred_element_type=jnp.float32
    )
    summed = reduce_rows(partial)
    gram = summed[:, :rank_count]
    cross = summed[:, rank_count:]
    lower_one, inverse = factor_and_invert(gram)
    scaled = jnp.dot(weighted, inverse.T, precision=HIGH) * root_points
    projected = jnp.dot(inverse, cross, precision=HIGH) * (math.sqrt(rank_count) / root_points)
    upper = lower_one.T / root_points
    return (scaled[None], upper[None], projected[None])


def solution(mesh):
    rows_n, batch_n = mesh.devices.shape
    along_x = len({d.coords[0] for d in mesh.devices.flat})
    along_y = len({d.coords[1] for d in mesh.devices.flat})
    devices = mesh.devices.reshape(along_x, rows_n // along_x, along_y, batch_n // along_y)
    fine = Mesh(devices, ("x", "z", "y", "core"))
    placed = (P(ROWS, BATCH), P(), P(), P(BATCH, None))
    return jax.shard_map(
        shards,
        mesh=fine,
        in_specs=placed,
        out_specs=(P(BATCH, ROWS, None), P(BATCH, None, None), P(BATCH, None, None)),
        check_vma=False,
    )
```

```python
import math

import jax
import jax.numpy as jnp
from jax import lax
from jax.experimental import pallas as pl
from jax.experimental.pallas import tpu as pltpu
from jax.sharding import Mesh
from jax.sharding import PartitionSpec as P

HIGH = lax.Precision.HIGHEST
ROWS = ("x", "z")
BATCH = ("y", "core")
BLOCK = 128


def shifted(x, axis, by):
    length = lax.axis_size(axis)
    pairs = [(i, i + by) for i in range(length) if 0 <= i + by < length]
    return lax.ppermute(x, axis, pairs)


def band_kernel(coefs_ref, inner_ref, carry_ref):
    row_ids = lax.broadcasted_iota(jnp.int32, (BLOCK, BLOCK), 0)
    col_ids = lax.broadcasted_iota(jnp.int32, (BLOCK, BLOCK), 1)
    lag_ids = col_ids - row_ids
    inner = jnp.zeros((BLOCK, BLOCK), jnp.float32)
    carry = jnp.zeros((BLOCK, BLOCK), jnp.float32)
    for k in range(coefs_ref.shape[0]):
        tap = coefs_ref[k]
        inner = jnp.where(lag_ids == k, tap, inner)
        carry = jnp.where(lag_ids == k - BLOCK, tap, carry)
    inner_ref[...] = inner.astype(inner_ref.dtype)
    carry_ref[...] = carry.astype(carry_ref.dtype)


def band_blocks(coefs):
    block = jax.ShapeDtypeStruct((BLOCK, BLOCK), jnp.bfloat16)
    vmem = pl.BlockSpec(memory_space=pltpu.VMEM)
    return pl.pallas_call(
        band_kernel,
        out_shape=(block, block),
        in_specs=[pl.BlockSpec(memory_space=pltpu.SMEM)],
        out_specs=(vmem, vmem),
    )(coefs)


def scatter_sum(flat, axis):
    count = lax.axis_size(axis)
    got = lax.all_to_all(flat.reshape(count, -1), axis, 0, 0, tiled=True)
    return jnp.sum(got, axis=0)


def gather_back(flat, axis):
    count = lax.axis_size(axis)
    spread = jnp.broadcast_to(flat[None], (count,) + flat.shape)
    return lax.all_to_all(spread, axis, 0, 0, tiled=True).reshape(-1)


def reduce_rows(x):
    flat = x.reshape(-1)
    flat = scatter_sum(flat, "x")
    flat = scatter_sum(flat, "z")
    flat = gather_back(flat, "z")
    flat = gather_back(flat, "x")
    return flat.reshape(x.shape)


def chol_kernel(g_ref, out_ref):
    n = g_ref.shape[0]
    rows = lax.broadcasted_iota(jnp.int32, (n, n), 0)
    cols = lax.broadcasted_iota(jnp.int32, (n, n), 1)
    whole = jnp.concatenate([g_ref[...], jnp.where(rows == cols, 1.0, 0.0).astype(jnp.float32)], axis=1)
    lane_row = lax.broadcasted_iota(jnp.int32, (1, 2 * n), 1)
    for j in range(n):
        lo = j - j % 8
        if j % 8 == 0 and j > 0:
            out_ref[lo - 8 : lo, :] = whole[:8]
            whole = whole[8:]
        r = j - lo
        row = whole[r : r + 1]
        scale = 1.0 / jnp.sqrt(row[:, j : j + 1])
        top = jnp.where(lane_row >= j, row * scale, 0.0)
        column = whole[:, j : j + 1] * scale
        sub = lax.broadcasted_iota(jnp.int32, whole.shape, 0)
        whole = jnp.where(sub > r, whole - column * top, jnp.where(sub == r, top, whole))
    out_ref[n - 8 :, :] = whole


def factor_block(g):
    n = g.shape[0]
    vmem = pl.BlockSpec(memory_space=pltpu.VMEM)
    out = pl.pallas_call(chol_kernel, out_shape=jax.ShapeDtypeStruct((n, 2 * n), jnp.float32),
        in_specs=[vmem], out_specs=vmem)(g)
    return out[:, :n].T, out[:, n:]


def factor_and_invert(gram):
    h = gram.shape[0] // 2
    l11, i11 = factor_block(gram[:h, :h])
    l21 = jnp.dot(gram[h:, :h], i11.T, precision=HIGH)
    l22, i22 = factor_block(gram[h:, h:] - jnp.dot(l21, l21.T, precision=HIGH))
    x21 = -jnp.dot(i22, jnp.dot(l21, i11, precision=HIGH), precision=HIGH)
    zero = jnp.zeros((h, h), jnp.float32)
    return jnp.block([[l11, zero], [l21, l22]]), jnp.block([[i11, zero], [x21, i22]])


def shards(frames, tap_table, sketch_matrix, decay_rates):
    rows_here, frame_count = frames.shape
    npoints = rows_here * math.prod(lax.axis_size(a) for a in ROWS)
    batch_count = lax.axis_size(BATCH)
    coefs = (tap_table.astype(jnp.float32) / 1024.0).astype(jnp.bfloat16).astype(jnp.float32)
    inner, carry = band_blocks(coefs)
    nblocks = frame_count // BLOCK
    zero = jnp.zeros((BLOCK, BLOCK), jnp.bfloat16)
    main_band = jnp.block(
        [[inner if j == i else (carry if j == i + 1 else zero) for j in range(nblocks)] for i in range(nblocks)]
    )
    history = shifted(frames[:, frame_count - BLOCK :], BATCH, 1)
    main = jnp.dot(frames, main_band, preferred_element_type=jnp.float32)
    edge = jnp.dot(history, carry, preferred_element_type=jnp.float32)
    filtered = (main + jnp.pad(edge, ((0, 0), (0, frame_count - BLOCK)))).astype(jnp.bfloat16)
    sketched = jnp.dot(filtered, sketch_matrix, preferred_element_type=jnp.float32)

    factors = []
    factor = decay_rates[0]
    d = 1
    while d < batch_count:
        factors.append(factor)
        factor = factor * shifted(factor, BATCH, d)
        d *= 2
    weighted = sketched
    d = 1
    for factor in factors:
        weighted = weighted + factor[None, :] * shifted(weighted, BATCH, d)
        d *= 2

    root_points = math.sqrt(npoints)
    rank_count = weighted.shape[1]
    both = jnp.concatenate([weighted, filtered.astype(jnp.float32)], axis=1)
    partial = lax.dot_general(
        weighted, both, (((0,), (0,)), ((), ())), precision=HIGH, preferred_element_type=jnp.float32
    )
    summed = reduce_rows(partial)
    gram = summed[:, :rank_count]
    cross = summed[:, rank_count:]
    lower_one, inverse = factor_and_invert(gram)
    scaled = jnp.dot(weighted, inverse.T, precision=HIGH) * root_points
    projected = jnp.dot(inverse, cross, precision=HIGH) * (math.sqrt(rank_count) / root_points)
    upper = lower_one.T / root_points
    return (scaled[None], upper[None], projected[None])


def solution(mesh):
    rows_n, batch_n = mesh.devices.shape
    along_x = len({d.coords[0] for d in mesh.devices.flat})
    along_y = len({d.coords[1] for d in mesh.devices.flat})
    devices = mesh.devices.reshape(along_x, rows_n // along_x, along_y, batch_n // along_y)
    fine = Mesh(devices, ("x", "z", "y", "core"))
    placed = (P(ROWS, BATCH), P(), P(), P(BATCH, None))
    return jax.shard_map(
        shards,
        mesh=fine,
        in_specs=placed,
        out_specs=(P(BATCH, ROWS, None), P(BATCH, None, None), P(BATCH, None, None)),
        check_vma=False,
    )
```

```python
import math

import jax
import jax.numpy as jnp
from jax import lax
from jax.experimental import pallas as pl
from jax.experimental.pallas import tpu as pltpu
from jax.sharding import Mesh
from jax.sharding import PartitionSpec as P

HIGH = lax.Precision.HIGHEST
ROWS = ("x", "z")
BATCH = ("y", "core")
BLOCK = 128


def shifted(x, axis, by):
    length = lax.axis_size(axis)
    pairs = [(i, i + by) for i in range(length) if 0 <= i + by < length]
    return lax.ppermute(x, axis, pairs)


def band_kernel(coefs_ref, inner_ref, carry_ref):
    row_ids = lax.broadcasted_iota(jnp.int32, (BLOCK, BLOCK), 0)
    col_ids = lax.broadcasted_iota(jnp.int32, (BLOCK, BLOCK), 1)
    lag_ids = col_ids - row_ids
    inner = jnp.zeros((BLOCK, BLOCK), jnp.float32)
    carry = jnp.zeros((BLOCK, BLOCK), jnp.float32)
    for k in range(coefs_ref.shape[0]):
        tap = coefs_ref[k]
        inner = jnp.where(lag_ids == k, tap, inner)
        carry = jnp.where(lag_ids == k - BLOCK, tap, carry)
    inner_ref[...] = inner.astype(inner_ref.dtype)
    carry_ref[...] = carry.astype(carry_ref.dtype)


def band_blocks(coefs):
    block = jax.ShapeDtypeStruct((BLOCK, BLOCK), jnp.bfloat16)
    vmem = pl.BlockSpec(memory_space=pltpu.VMEM)
    return pl.pallas_call(
        band_kernel,
        out_shape=(block, block),
        in_specs=[pl.BlockSpec(memory_space=pltpu.SMEM)],
        out_specs=(vmem, vmem),
    )(coefs)


def scatter_sum(flat, axis):
    count = lax.axis_size(axis)
    got = lax.all_to_all(flat.reshape(count, -1), axis, 0, 0, tiled=True)
    return jnp.sum(got, axis=0)


def gather_back(flat, axis):
    count = lax.axis_size(axis)
    spread = jnp.broadcast_to(flat[None], (count,) + flat.shape)
    return lax.all_to_all(spread, axis, 0, 0, tiled=True).reshape(-1)


def reduce_rows(x):
    flat = x.reshape(-1)
    flat = scatter_sum(flat, "x")
    flat = scatter_sum(flat, "z")
    flat = gather_back(flat, "z")
    flat = gather_back(flat, "x")
    return flat.reshape(x.shape)


def chol_kernel(g_ref, out_ref):
    n = g_ref.shape[0]
    rows = lax.broadcasted_iota(jnp.int32, (n, n), 0)
    cols = lax.broadcasted_iota(jnp.int32, (n, n), 1)
    whole = jnp.concatenate([g_ref[...], jnp.where(rows == cols, 1.0, 0.0).astype(jnp.float32)], axis=1)
    lane_row = lax.broadcasted_iota(jnp.int32, (1, 2 * n), 1)
    for j in range(n):
        lo = j - j % 8
        if j % 8 == 0 and j > 0:
            out_ref[lo - 8 : lo, :] = whole[:8]
            whole = whole[8:]
        r = j - lo
        row = whole[r : r + 1]
        inverse = 1.0 / row[:, j : j + 1]
        kept = jnp.where(lane_row >= j, row, 0.0)
        top = kept * jnp.sqrt(inverse)
        sub = lax.broadcasted_iota(jnp.int32, whole.shape, 0)
        whole = jnp.where(
            sub > r, whole - whole[:, j : j + 1] * (kept * inverse), jnp.where(sub == r, top, whole)
        )
    out_ref[n - 8 :, :] = whole


def factor_block(g):
    n = g.shape[0]
    vmem = pl.BlockSpec(memory_space=pltpu.VMEM)
    out = pl.pallas_call(chol_kernel, out_shape=jax.ShapeDtypeStruct((n, 2 * n), jnp.float32),
        in_specs=[vmem], out_specs=vmem)(g)
    return out[:, :n].T, out[:, n:]


def factor_and_invert(gram):
    h = gram.shape[0] // 2
    l11, i11 = factor_block(gram[:h, :h])
    l21 = jnp.dot(gram[h:, :h], i11.T, precision=HIGH)
    l22, i22 = factor_block(gram[h:, h:] - jnp.dot(l21, l21.T, precision=HIGH))
    x21 = -jnp.dot(i22, jnp.dot(l21, i11, precision=HIGH), precision=HIGH)
    zero = jnp.zeros((h, h), jnp.float32)
    return jnp.block([[l11, zero], [l21, l22]]), jnp.block([[i11, zero], [x21, i22]])


def shards(frames, tap_table, sketch_matrix, decay_rates):
    rows_here, frame_count = frames.shape
    npoints = rows_here * math.prod(lax.axis_size(a) for a in ROWS)
    batch_count = lax.axis_size(BATCH)
    coefs = (tap_table.astype(jnp.float32) / 1024.0).astype(jnp.bfloat16).astype(jnp.float32)
    inner, carry = band_blocks(coefs)
    nblocks = frame_count // BLOCK
    zero = jnp.zeros((BLOCK, BLOCK), jnp.bfloat16)
    main_band = jnp.block(
        [[inner if j == i else (carry if j == i + 1 else zero) for j in range(nblocks)] for i in range(nblocks)]
    )
    history = shifted(frames[:, frame_count - BLOCK :], BATCH, 1)
    main = jnp.dot(frames, main_band, preferred_element_type=jnp.float32)
    edge = jnp.dot(history, carry, preferred_element_type=jnp.float32)
    filtered = (main + jnp.pad(edge, ((0, 0), (0, frame_count - BLOCK)))).astype(jnp.bfloat16)
    sketched = jnp.dot(filtered, sketch_matrix, preferred_element_type=jnp.float32)

    factors = []
    factor = decay_rates[0]
    d = 1
    while d < batch_count:
        factors.append(factor)
        factor = factor * shifted(factor, BATCH, d)
        d *= 2
    weighted = sketched
    d = 1
    for factor in factors:
        weighted = weighted + factor[None, :] * shifted(weighted, BATCH, d)
        d *= 2

    root_points = math.sqrt(npoints)
    rank_count = weighted.shape[1]
    both = jnp.concatenate([weighted, filtered.astype(jnp.float32)], axis=1)
    partial = lax.dot_general(
        weighted, both, (((0,), (0,)), ((), ())), precision=HIGH, preferred_element_type=jnp.float32
    )
    summed = reduce_rows(partial)
    gram = summed[:, :rank_count]
    cross = summed[:, rank_count:]
    lower_one, inverse = factor_and_invert(gram)
    scaled = jnp.dot(weighted, inverse.T, precision=HIGH) * root_points
    projected = jnp.dot(inverse, cross, precision=HIGH) * (math.sqrt(rank_count) / root_points)
    upper = lower_one.T / root_points
    return (scaled[None], upper[None], projected[None])


def solution(mesh):
    rows_n, batch_n = mesh.devices.shape
    along_x = len({d.coords[0] for d in mesh.devices.flat})
    along_y = len({d.coords[1] for d in mesh.devices.flat})
    devices = mesh.devices.reshape(along_x, rows_n // along_x, along_y, batch_n // along_y)
    fine = Mesh(devices, ("x", "z", "y", "core"))
    placed = (P(ROWS, BATCH), P(), P(), P(BATCH, None))
    return jax.shard_map(
        shards,
        mesh=fine,
        in_specs=placed,
        out_specs=(P(BATCH, ROWS, None), P(BATCH, None, None), P(BATCH, None, None)),
        check_vma=False,
    )
```

```python
import math

import jax
import jax.numpy as jnp
from jax import lax
from jax.experimental import pallas as pl
from jax.experimental.pallas import tpu as pltpu
from jax.sharding import Mesh
from jax.sharding import PartitionSpec as P

HIGH = lax.Precision.HIGHEST
ROWS = ("x", "z")
BATCH = ("y", "core")
BLOCK = 128


def shifted(x, axis, by):
    length = lax.axis_size(axis)
    pairs = [(i, i + by) for i in range(length) if 0 <= i + by < length]
    return lax.ppermute(x, axis, pairs)


def band_kernel(coefs_ref, inner_ref, carry_ref):
    row_ids = lax.broadcasted_iota(jnp.int32, (BLOCK, BLOCK), 0)
    col_ids = lax.broadcasted_iota(jnp.int32, (BLOCK, BLOCK), 1)
    lag_ids = col_ids - row_ids
    inner = jnp.zeros((BLOCK, BLOCK), jnp.float32)
    carry = jnp.zeros((BLOCK, BLOCK), jnp.float32)
    for k in range(coefs_ref.shape[0]):
        tap = coefs_ref[k]
        inner = jnp.where(lag_ids == k, tap, inner)
        carry = jnp.where(lag_ids == k - BLOCK, tap, carry)
    inner_ref[...] = inner.astype(inner_ref.dtype)
    carry_ref[...] = carry.astype(carry_ref.dtype)


def band_blocks(coefs):
    block = jax.ShapeDtypeStruct((BLOCK, BLOCK), jnp.bfloat16)
    vmem = pl.BlockSpec(memory_space=pltpu.VMEM)
    return pl.pallas_call(
        band_kernel,
        out_shape=(block, block),
        in_specs=[pl.BlockSpec(memory_space=pltpu.SMEM)],
        out_specs=(vmem, vmem),
    )(coefs)


def scatter_sum(flat, axis):
    count = lax.axis_size(axis)
    got = lax.all_to_all(flat.reshape(count, -1), axis, 0, 0, tiled=True)
    return jnp.sum(got, axis=0)


def gather_back(flat, axis):
    count = lax.axis_size(axis)
    spread = jnp.broadcast_to(flat[None], (count,) + flat.shape)
    return lax.all_to_all(spread, axis, 0, 0, tiled=True).reshape(-1)


def reduce_rows(x):
    flat = x.reshape(-1)
    flat = scatter_sum(flat, "x")
    flat = scatter_sum(flat, "z")
    flat = gather_back(flat, "z")
    flat = gather_back(flat, "x")
    return flat.reshape(x.shape)


def chol_kernel(g_ref, out_ref):
    n = g_ref.shape[0]
    rows = lax.broadcasted_iota(jnp.int32, (n, n), 0)
    cols = lax.broadcasted_iota(jnp.int32, (n, n), 1)
    whole = jnp.concatenate([g_ref[...], jnp.where(rows == cols, 1.0, 0.0).astype(jnp.float32)], axis=1)
    lane_row = lax.broadcasted_iota(jnp.int32, (1, 2 * n), 1)
    for j in range(n):
        lo = j - j % 8
        if j % 8 == 0 and j > 0:
            out_ref[lo - 8 : lo, :] = whole[:8]
            whole = whole[8:]
        r = j - lo
        row = whole[r : r + 1]
        inverse = 1.0 / row[:, j : j + 1]
        kept = jnp.where(lane_row >= j, row, 0.0)
        top = kept * jnp.sqrt(inverse)
        sub = lax.broadcasted_iota(jnp.int32, whole.shape, 0)
        whole = jnp.where(
            sub > r, whole - whole[:, j : j + 1] * (kept * inverse), jnp.where(sub == r, top, whole)
        )
    out_ref[n - 8 :, :] = whole


def factor_block(g):
    n = g.shape[0]
    vmem = pl.BlockSpec(memory_space=pltpu.VMEM)
    out = pl.pallas_call(chol_kernel, out_shape=jax.ShapeDtypeStruct((n, 2 * n), jnp.float32),
        in_specs=[vmem], out_specs=vmem)(g)
    return out[:, :n].T, out[:, n:]


def shards(frames, tap_table, sketch_matrix, decay_rates):
    rows_here, frame_count = frames.shape
    npoints = rows_here * math.prod(lax.axis_size(a) for a in ROWS)
    batch_count = lax.axis_size(BATCH)
    coefs = (tap_table.astype(jnp.float32) / 1024.0).astype(jnp.bfloat16).astype(jnp.float32)
    inner, carry = band_blocks(coefs)
    nblocks = frame_count // BLOCK
    zero = jnp.zeros((BLOCK, BLOCK), jnp.bfloat16)
    main_band = jnp.block(
        [[inner if j == i else (carry if j == i + 1 else zero) for j in range(nblocks)] for i in range(nblocks)]
    )
    history = shifted(frames[:, frame_count - BLOCK :], BATCH, 1)
    main = jnp.dot(frames, main_band, preferred_element_type=jnp.float32)
    edge = jnp.dot(history, carry, preferred_element_type=jnp.float32)
    filtered = (main + jnp.pad(edge, ((0, 0), (0, frame_count - BLOCK)))).astype(jnp.bfloat16)
    sketched = jnp.dot(filtered, sketch_matrix, preferred_element_type=jnp.float32)

    factors = []
    factor = decay_rates[0]
    d = 1
    while d < batch_count:
        factors.append(factor)
        factor = factor * shifted(factor, BATCH, d)
        d *= 2
    weighted = sketched
    d = 1
    for factor in factors:
        weighted = weighted + factor[None, :] * shifted(weighted, BATCH, d)
        d *= 2

    root_points = math.sqrt(npoints)
    rank_count = weighted.shape[1]
    both = jnp.concatenate([weighted, filtered.astype(jnp.float32)], axis=1)
    partial = lax.dot_general(
        weighted, both, (((0,), (0,)), ((), ())), precision=HIGH, preferred_element_type=jnp.float32
    )
    summed = reduce_rows(partial)
    gram = summed[:, :rank_count]
    cross = summed[:, rank_count:]
    lower_one, inverse = factor_block(gram)
    scaled = jnp.dot(weighted, inverse.T, precision=HIGH) * root_points
    projected = jnp.dot(inverse, cross, precision=HIGH) * (math.sqrt(rank_count) / root_points)
    upper = lower_one.T / root_points
    return (scaled[None], upper[None], projected[None])


def solution(mesh):
    rows_n, batch_n = mesh.devices.shape
    along_x = len({d.coords[0] for d in mesh.devices.flat})
    along_y = len({d.coords[1] for d in mesh.devices.flat})
    devices = mesh.devices.reshape(along_x, rows_n // along_x, along_y, batch_n // along_y)
    fine = Mesh(devices, ("x", "z", "y", "core"))
    placed = (P(ROWS, BATCH), P(), P(), P(BATCH, None))
    return jax.shard_map(
        shards,
        mesh=fine,
        in_specs=placed,
        out_specs=(P(BATCH, ROWS, None), P(BATCH, None, None), P(BATCH, None, None)),
        check_vma=False,
    )
```

```python
import math

import jax
import jax.numpy as jnp
from jax import lax
from jax.experimental import pallas as pl
from jax.experimental.pallas import tpu as pltpu
from jax.sharding import Mesh
from jax.sharding import PartitionSpec as P

HIGH = lax.Precision.HIGHEST
ROWS = ("x", "z")
BATCH = ("y", "core")
BLOCK = 128


def shifted(x, axis, by):
    length = lax.axis_size(axis)
    pairs = [(i, i + by) for i in range(length) if 0 <= i + by < length]
    return lax.ppermute(x, axis, pairs)


def band_kernel(coefs_ref, inner_ref, carry_ref):
    row_ids = lax.broadcasted_iota(jnp.int32, (BLOCK, BLOCK), 0)
    col_ids = lax.broadcasted_iota(jnp.int32, (BLOCK, BLOCK), 1)
    lag_ids = col_ids - row_ids
    inner = jnp.zeros((BLOCK, BLOCK), jnp.float32)
    carry = jnp.zeros((BLOCK, BLOCK), jnp.float32)
    for k in range(coefs_ref.shape[0]):
        tap = coefs_ref[k]
        inner = jnp.where(lag_ids == k, tap, inner)
        carry = jnp.where(lag_ids == k - BLOCK, tap, carry)
    inner_ref[...] = inner.astype(inner_ref.dtype)
    carry_ref[...] = carry.astype(carry_ref.dtype)


def band_blocks(coefs):
    block = jax.ShapeDtypeStruct((BLOCK, BLOCK), jnp.bfloat16)
    vmem = pl.BlockSpec(memory_space=pltpu.VMEM)
    return pl.pallas_call(
        band_kernel,
        out_shape=(block, block),
        in_specs=[pl.BlockSpec(memory_space=pltpu.SMEM)],
        out_specs=(vmem, vmem),
    )(coefs)


def scatter_sum(flat, axis):
    count = lax.axis_size(axis)
    got = lax.all_to_all(flat.reshape(count, -1), axis, 0, 0, tiled=True)
    return jnp.sum(got, axis=0)


def gather_back(flat, axis):
    count = lax.axis_size(axis)
    spread = jnp.broadcast_to(flat[None], (count,) + flat.shape)
    return lax.all_to_all(spread, axis, 0, 0, tiled=True).reshape(-1)


def reduce_rows(x):
    flat = x.reshape(-1)
    flat = scatter_sum(flat, "x")
    flat = scatter_sum(flat, "z")
    flat = gather_back(flat, "z")
    flat = gather_back(flat, "x")
    return flat.reshape(x.shape)


def chol_kernel(g_ref, out_ref):
    n = g_ref.shape[0]
    rows = lax.broadcasted_iota(jnp.int32, (n, n), 0)
    cols = lax.broadcasted_iota(jnp.int32, (n, n), 1)
    whole = jnp.concatenate([g_ref[...], jnp.where(rows == cols, 1.0, 0.0).astype(jnp.float32)], axis=1)
    lane_row = lax.broadcasted_iota(jnp.int32, (1, 2 * n), 1)
    for j in range(0, n, 2):
        lo = j - j % 8
        if j % 8 == 0 and j > 0:
            out_ref[lo - 8 : lo, :] = whole[:8]
            whole = whole[8:]
        r = j - lo
        first = jnp.where(lane_row >= j, whole[r : r + 1], 0.0)
        inverse = 1.0 / first[:, j : j + 1]
        first_scaled = first * inverse
        second_row = whole[r + 1 : r + 2]
        second = jnp.where(lane_row >= j + 1, second_row - second_row[:, j : j + 1] * first_scaled, 0.0)
        inverse_2 = 1.0 / second[:, j + 1 : j + 2]
        column = whole[:, j : j + 1]
        column_2 = whole[:, j + 1 : j + 2] - column * first_scaled[:, j + 1 : j + 2]
        sub = lax.broadcasted_iota(jnp.int32, whole.shape, 0)
        rest = whole - column * first_scaled - column_2 * (second * inverse_2)
        whole = jnp.where(
            sub > r + 1,
            rest,
            jnp.where(
                sub == r,
                first * jnp.sqrt(inverse),
                jnp.where(sub == r + 1, second * jnp.sqrt(inverse_2), whole),
            ),
        )
    out_ref[n - 8 :, :] = whole


def factor_block(g):
    n = g.shape[0]
    vmem = pl.BlockSpec(memory_space=pltpu.VMEM)
    out = pl.pallas_call(chol_kernel, out_shape=jax.ShapeDtypeStruct((n, 2 * n), jnp.float32),
        in_specs=[vmem], out_specs=vmem)(g)
    return out[:, :n].T, out[:, n:]


def shards(frames, tap_table, sketch_matrix, decay_rates):
    rows_here, frame_count = frames.shape
    npoints = rows_here * math.prod(lax.axis_size(a) for a in ROWS)
    batch_count = lax.axis_size(BATCH)
    coefs = (tap_table.astype(jnp.float32) / 1024.0).astype(jnp.bfloat16).astype(jnp.float32)
    inner, carry = band_blocks(coefs)
    nblocks = frame_count // BLOCK
    zero = jnp.zeros((BLOCK, BLOCK), jnp.bfloat16)
    main_band = jnp.block(
        [[inner if j == i else (carry if j == i + 1 else zero) for j in range(nblocks)] for i in range(nblocks)]
    )
    history = shifted(frames[:, frame_count - BLOCK :], BATCH, 1)
    main = jnp.dot(frames, main_band, preferred_element_type=jnp.float32)
    edge = jnp.dot(history, carry, preferred_element_type=jnp.float32)
    filtered = (main + jnp.pad(edge, ((0, 0), (0, frame_count - BLOCK)))).astype(jnp.bfloat16)
    sketched = jnp.dot(filtered, sketch_matrix, preferred_element_type=jnp.float32)

    factors = []
    factor = decay_rates[0]
    d = 1
    while d < batch_count:
        factors.append(factor)
        factor = factor * shifted(factor, BATCH, d)
        d *= 2
    weighted = sketched
    d = 1
    for factor in factors:
        weighted = weighted + factor[None, :] * shifted(weighted, BATCH, d)
        d *= 2

    root_points = math.sqrt(npoints)
    rank_count = weighted.shape[1]
    both = jnp.concatenate([weighted, filtered.astype(jnp.float32)], axis=1)
    partial = lax.dot_general(
        weighted, both, (((0,), (0,)), ((), ())), precision=HIGH, preferred_element_type=jnp.float32
    )
    summed = reduce_rows(partial)
    gram = summed[:, :rank_count]
    cross = summed[:, rank_count:]
    lower_one, inverse = factor_block(gram)
    scaled = jnp.dot(weighted, inverse.T, precision=HIGH) * root_points
    projected = jnp.dot(inverse, cross, precision=HIGH) * (math.sqrt(rank_count) / root_points)
    upper = lower_one.T / root_points
    return (scaled[None], upper[None], projected[None])


def solution(mesh):
    rows_n, batch_n = mesh.devices.shape
    along_x = len({d.coords[0] for d in mesh.devices.flat})
    along_y = len({d.coords[1] for d in mesh.devices.flat})
    devices = mesh.devices.reshape(along_x, rows_n // along_x, along_y, batch_n // along_y)
    fine = Mesh(devices, ("x", "z", "y", "core"))
    placed = (P(ROWS, BATCH), P(), P(), P(BATCH, None))
    return jax.shard_map(
        shards,
        mesh=fine,
        in_specs=placed,
        out_specs=(P(BATCH, ROWS, None), P(BATCH, None, None), P(BATCH, None, None)),
        check_vma=False,
    )
```

```python
import math

import jax
import jax.numpy as jnp
from jax import lax
from jax.experimental import pallas as pl
from jax.experimental.pallas import tpu as pltpu
from jax.sharding import Mesh
from jax.sharding import PartitionSpec as P

HIGH = lax.Precision.HIGHEST
ROWS = ("x", "z")
BATCH = ("y", "core")
BLOCK = 128


def shifted(x, axis, by):
    length = lax.axis_size(axis)
    pairs = [(i, i + by) for i in range(length) if 0 <= i + by < length]
    return lax.ppermute(x, axis, pairs)


def band_kernel(coefs_ref, inner_ref, carry_ref):
    row_ids = lax.broadcasted_iota(jnp.int32, (BLOCK, BLOCK), 0)
    col_ids = lax.broadcasted_iota(jnp.int32, (BLOCK, BLOCK), 1)
    lag_ids = col_ids - row_ids
    inner = jnp.zeros((BLOCK, BLOCK), jnp.float32)
    carry = jnp.zeros((BLOCK, BLOCK), jnp.float32)
    for k in range(coefs_ref.shape[0]):
        tap = coefs_ref[k]
        inner = jnp.where(lag_ids == k, tap, inner)
        carry = jnp.where(lag_ids == k - BLOCK, tap, carry)
    inner_ref[...] = inner.astype(inner_ref.dtype)
    carry_ref[...] = carry.astype(carry_ref.dtype)


def band_blocks(coefs):
    block = jax.ShapeDtypeStruct((BLOCK, BLOCK), jnp.bfloat16)
    vmem = pl.BlockSpec(memory_space=pltpu.VMEM)
    return pl.pallas_call(
        band_kernel,
        out_shape=(block, block),
        in_specs=[pl.BlockSpec(memory_space=pltpu.SMEM)],
        out_specs=(vmem, vmem),
    )(coefs)


def scatter_sum(flat, axis):
    count = lax.axis_size(axis)
    got = lax.all_to_all(flat.reshape(count, -1), axis, 0, 0, tiled=True)
    return jnp.sum(got, axis=0)


def gather_back(flat, axis):
    count = lax.axis_size(axis)
    spread = jnp.broadcast_to(flat[None], (count,) + flat.shape)
    return lax.all_to_all(spread, axis, 0, 0, tiled=True).reshape(-1)


def reduce_rows(x):
    flat = x.reshape(-1)
    flat = scatter_sum(flat, "x")
    flat = scatter_sum(flat, "z")
    flat = gather_back(flat, "z")
    flat = gather_back(flat, "x")
    return flat.reshape(x.shape)


def chol_kernel(g_ref, out_ref):
    n = g_ref.shape[0]
    rows = lax.broadcasted_iota(jnp.int32, (n, n), 0)
    cols = lax.broadcasted_iota(jnp.int32, (n, n), 1)
    whole = jnp.concatenate([g_ref[...], jnp.where(rows == cols, 1.0, 0.0).astype(jnp.float32)], axis=1)
    lane_row = lax.broadcasted_iota(jnp.int32, (1, 2 * n), 1)
    for j in range(n):
        lo = j - j % 8
        if j % 8 == 0 and j > 0:
            out_ref[lo - 8 : lo, :] = whole[:8]
            whole = whole[8:]
        r = j - lo
        row = whole[r : r + 1]
        inverse = 1.0 / row[:, j : j + 1]
        kept = jnp.where(lane_row >= j, row, 0.0)
        top = kept * jnp.sqrt(inverse)
        sub = lax.broadcasted_iota(jnp.int32, whole.shape, 0)
        whole = jnp.where(
            sub > r, whole - whole[:, j : j + 1] * (kept * inverse), jnp.where(sub == r, top, whole)
        )
    out_ref[n - 8 :, :] = whole


def factor_block(g):
    n = g.shape[0]
    vmem = pl.BlockSpec(memory_space=pltpu.VMEM)
    out = pl.pallas_call(chol_kernel, out_shape=jax.ShapeDtypeStruct((n, 2 * n), jnp.float32),
        in_specs=[vmem], out_specs=vmem)(g)
    return out[:, :n].T, out[:, n:]


def shards(frames, tap_table, sketch_matrix, decay_rates):
    rows_here, frame_count = frames.shape
    npoints = rows_here * math.prod(lax.axis_size(a) for a in ROWS)
    batch_count = lax.axis_size(BATCH)
    coefs = (tap_table.astype(jnp.float32) / 1024.0).astype(jnp.bfloat16).astype(jnp.float32)
    inner, carry = band_blocks(coefs)
    nblocks = frame_count // BLOCK
    zero = jnp.zeros((BLOCK, BLOCK), jnp.bfloat16)
    main_band = jnp.block(
        [[inner if j == i else (carry if j == i + 1 else zero) for j in range(nblocks)] for i in range(nblocks)]
    )
    history = shifted(frames[:, frame_count - BLOCK :], BATCH, 1)
    main = jnp.dot(frames, main_band, preferred_element_type=jnp.float32)
    edge = jnp.dot(history, carry, preferred_element_type=jnp.float32)
    filtered = (main + jnp.pad(edge, ((0, 0), (0, frame_count - BLOCK)))).astype(jnp.bfloat16)
    sketched = jnp.dot(filtered, sketch_matrix, preferred_element_type=jnp.float32)

    factors = []
    factor = decay_rates[0]
    d = 1
    while d < batch_count:
        factors.append(factor)
        factor = factor * shifted(factor, BATCH, d)
        d *= 2
    weighted = sketched
    d = 1
    for factor in factors:
        weighted = weighted + factor[None, :] * shifted(weighted, BATCH, d)
        d *= 2

    root_points = math.sqrt(npoints)
    rank_count = weighted.shape[1]
    both = jnp.concatenate([weighted, filtered.astype(jnp.float32)], axis=1)
    partial = lax.dot_general(
        weighted, both, (((0,), (0,)), ((), ())), precision=HIGH, preferred_element_type=jnp.float32
    )
    h = rank_count // 2
    pieces = (partial[:h, :rank_count], partial[h:, h:rank_count], partial[:, rank_count:])
    summed = reduce_rows(jnp.concatenate([p.reshape(-1) for p in pieces]))
    upper_rows = summed[: h * rank_count].reshape(h, rank_count)
    corner = summed[h * rank_count : h * rank_count + h * h].reshape(h, h)
    cross = summed[h * rank_count + h * h :].reshape(rank_count, -1)
    gram = jnp.concatenate([upper_rows, jnp.concatenate([upper_rows[:, h:].T, corner], axis=1)], axis=0)
    lower_one, inverse = factor_block(gram)
    scaled = jnp.dot(weighted, inverse.T, precision=HIGH) * root_points
    projected = jnp.dot(inverse, cross, precision=HIGH) * (math.sqrt(rank_count) / root_points)
    upper = lower_one.T / root_points
    return (scaled[None], upper[None], projected[None])


def solution(mesh):
    rows_n, batch_n = mesh.devices.shape
    along_x = len({d.coords[0] for d in mesh.devices.flat})
    along_y = len({d.coords[1] for d in mesh.devices.flat})
    devices = mesh.devices.reshape(along_x, rows_n // along_x, along_y, batch_n // along_y)
    fine = Mesh(devices, ("x", "z", "y", "core"))
    placed = (P(ROWS, BATCH), P(), P(), P(BATCH, None))
    return jax.shard_map(
        shards,
        mesh=fine,
        in_specs=placed,
        out_specs=(P(BATCH, ROWS, None), P(BATCH, None, None), P(BATCH, None, None)),
        check_vma=False,
    )
```

```python
import math

import jax
import jax.numpy as jnp
from jax import lax
from jax.experimental import pallas as pl
from jax.experimental.pallas import tpu as pltpu
from jax.sharding import Mesh
from jax.sharding import PartitionSpec as P

HIGH = lax.Precision.HIGHEST
ROWS = ("x", "z")
BATCH = ("y", "core")
BLOCK = 128


def shifted(x, axis, by):
    length = lax.axis_size(axis)
    pairs = [(i, i + by) for i in range(length) if 0 <= i + by < length]
    return lax.ppermute(x, axis, pairs)


def band_kernel(coefs_ref, inner_ref, carry_ref):
    row_ids = lax.broadcasted_iota(jnp.int32, (BLOCK, BLOCK), 0)
    col_ids = lax.broadcasted_iota(jnp.int32, (BLOCK, BLOCK), 1)
    lag_ids = col_ids - row_ids
    inner = jnp.zeros((BLOCK, BLOCK), jnp.float32)
    carry = jnp.zeros((BLOCK, BLOCK), jnp.float32)
    for k in range(coefs_ref.shape[0]):
        tap = coefs_ref[k]
        inner = jnp.where(lag_ids == k, tap, inner)
        carry = jnp.where(lag_ids == k - BLOCK, tap, carry)
    inner_ref[...] = inner.astype(inner_ref.dtype)
    carry_ref[...] = carry.astype(carry_ref.dtype)


def band_blocks(coefs):
    block = jax.ShapeDtypeStruct((BLOCK, BLOCK), jnp.bfloat16)
    vmem = pl.BlockSpec(memory_space=pltpu.VMEM)
    return pl.pallas_call(
        band_kernel,
        out_shape=(block, block),
        in_specs=[pl.BlockSpec(memory_space=pltpu.SMEM)],
        out_specs=(vmem, vmem),
    )(coefs)


def scatter_sum(flat, axis):
    count = lax.axis_size(axis)
    got = lax.all_to_all(flat.reshape(count, -1), axis, 0, 0, tiled=True)
    return jnp.sum(got, axis=0)


def gather_back(flat, axis):
    count = lax.axis_size(axis)
    spread = jnp.broadcast_to(flat[None], (count,) + flat.shape)
    return lax.all_to_all(spread, axis, 0, 0, tiled=True).reshape(-1)


def reduce_rows(x):
    flat = x.reshape(-1)
    flat = scatter_sum(flat, "x")
    flat = scatter_sum(flat, "z")
    flat = gather_back(flat, "z")
    flat = gather_back(flat, "x")
    return flat.reshape(x.shape)


def chol_kernel(g_ref, out_ref):
    n = g_ref.shape[0]
    rows = lax.broadcasted_iota(jnp.int32, (n, n), 0)
    cols = lax.broadcasted_iota(jnp.int32, (n, n), 1)
    whole = jnp.concatenate([g_ref[...], jnp.where(rows == cols, 1.0, 0.0).astype(jnp.float32)], axis=1)
    lane_row = lax.broadcasted_iota(jnp.int32, (1, 2 * n), 1)
    for j in range(n):
        lo = j - j % 8
        if j % 8 == 0 and j > 0:
            out_ref[lo - 8 : lo, :] = whole[:8]
            whole = whole[8:]
        r = j - lo
        row = whole[r : r + 1]
        inverse = 1.0 / row[:, j : j + 1]
        kept = jnp.where(lane_row >= j, row, 0.0)
        top = kept * jnp.sqrt(inverse)
        sub = lax.broadcasted_iota(jnp.int32, whole.shape, 0)
        whole = jnp.where(
            sub > r, whole - whole[:, j : j + 1] * (kept * inverse), jnp.where(sub == r, top, whole)
        )
    out_ref[n - 8 :, :] = whole


def factor_block(g):
    n = g.shape[0]
    vmem = pl.BlockSpec(memory_space=pltpu.VMEM)
    out = pl.pallas_call(chol_kernel, out_shape=jax.ShapeDtypeStruct((n, 2 * n), jnp.float32),
        in_specs=[vmem], out_specs=vmem)(g)
    return out[:, :n].T, out[:, n:]


def shards(frames, tap_table, sketch_matrix, decay_rates):
    rows_here, frame_count = frames.shape
    npoints = rows_here * math.prod(lax.axis_size(a) for a in ROWS)
    batch_count = lax.axis_size(BATCH)
    coefs = (tap_table.astype(jnp.float32) / 1024.0).astype(jnp.bfloat16).astype(jnp.float32)
    inner, carry = band_blocks(coefs)
    nblocks = frame_count // BLOCK
    zero = jnp.zeros((BLOCK, BLOCK), jnp.bfloat16)
    main_band = jnp.block(
        [[inner if j == i else (carry if j == i + 1 else zero) for j in range(nblocks)] for i in range(nblocks)]
    )
    history = shifted(frames[:, frame_count - BLOCK :], BATCH, 1)
    main = jnp.dot(frames, main_band, preferred_element_type=jnp.float32)
    edge = jnp.dot(history, carry, preferred_element_type=jnp.float32)
    filtered = (main + jnp.pad(edge, ((0, 0), (0, frame_count - BLOCK)))).astype(jnp.bfloat16)
    sketched = jnp.dot(filtered, sketch_matrix, preferred_element_type=jnp.float32)

    factors = []
    factor = decay_rates[0]
    d = 1
    while d < batch_count:
        factors.append(factor)
        factor = factor * shifted(factor, BATCH, d)
        d *= 2
    weighted = sketched
    d = 1
    for factor in factors:
        weighted = weighted + factor[None, :] * shifted(weighted, BATCH, d)
        d *= 2

    root_points = math.sqrt(npoints)
    rank_count = weighted.shape[1]
    both = jnp.concatenate([weighted, filtered.astype(jnp.float32)], axis=1)
    partial = lax.dot_general(
        weighted, both, (((0,), (0,)), ((), ())), precision=HIGH, preferred_element_type=jnp.float32
    )
    summed = reduce_rows(partial)
    gram = summed[:, :rank_count]
    cross = summed[:, rank_count:]
    lower_one, inverse = factor_block(gram)
    scaled = jnp.dot(weighted, inverse.T, precision=lax.Precision.HIGH) * root_points
    projected = jnp.dot(inverse, cross, precision=lax.Precision.HIGH) * (math.sqrt(rank_count) / root_points)
    upper = lower_one.T / root_points
    return (scaled[None], upper[None], projected[None])


def solution(mesh):
    rows_n, batch_n = mesh.devices.shape
    along_x = len({d.coords[0] for d in mesh.devices.flat})
    along_y = len({d.coords[1] for d in mesh.devices.flat})
    devices = mesh.devices.reshape(along_x, rows_n // along_x, along_y, batch_n // along_y)
    fine = Mesh(devices, ("x", "z", "y", "core"))
    placed = (P(ROWS, BATCH), P(), P(), P(BATCH, None))
    return jax.shard_map(
        shards,
        mesh=fine,
        in_specs=placed,
        out_specs=(P(BATCH, ROWS, None), P(BATCH, None, None), P(BATCH, None, None)),
        check_vma=False,
    )
```

```python
import math

import jax
import jax.numpy as jnp
from jax import lax
from jax.experimental import pallas as pl
from jax.experimental.pallas import tpu as pltpu
from jax.sharding import Mesh
from jax.sharding import PartitionSpec as P

HIGH = lax.Precision.HIGHEST
ROWS = ("x", "z")
BATCH = ("y", "core")
BLOCK = 128


def shifted(x, axis, by):
    length = lax.axis_size(axis)
    pairs = [(i, i + by) for i in range(length) if 0 <= i + by < length]
    return lax.ppermute(x, axis, pairs)


def band_kernel(coefs_ref, inner_ref, carry_ref):
    row_ids = lax.broadcasted_iota(jnp.int32, (BLOCK, BLOCK), 0)
    col_ids = lax.broadcasted_iota(jnp.int32, (BLOCK, BLOCK), 1)
    lag_ids = col_ids - row_ids
    inner = jnp.zeros((BLOCK, BLOCK), jnp.float32)
    carry = jnp.zeros((BLOCK, BLOCK), jnp.float32)
    for k in range(coefs_ref.shape[0]):
        tap = coefs_ref[k]
        inner = jnp.where(lag_ids == k, tap, inner)
        carry = jnp.where(lag_ids == k - BLOCK, tap, carry)
    inner_ref[...] = inner.astype(inner_ref.dtype)
    carry_ref[...] = carry.astype(carry_ref.dtype)


def band_blocks(coefs):
    block = jax.ShapeDtypeStruct((BLOCK, BLOCK), jnp.bfloat16)
    vmem = pl.BlockSpec(memory_space=pltpu.VMEM)
    return pl.pallas_call(
        band_kernel,
        out_shape=(block, block),
        in_specs=[pl.BlockSpec(memory_space=pltpu.SMEM)],
        out_specs=(vmem, vmem),
    )(coefs)


def scatter_sum(flat, axis):
    count = lax.axis_size(axis)
    got = lax.all_to_all(flat.reshape(count, -1), axis, 0, 0, tiled=True)
    return jnp.sum(got, axis=0)


def gather_back(flat, axis):
    count = lax.axis_size(axis)
    spread = jnp.broadcast_to(flat[None], (count,) + flat.shape)
    return lax.all_to_all(spread, axis, 0, 0, tiled=True).reshape(-1)


def reduce_rows(x):
    flat = x.reshape(-1)
    flat = scatter_sum(flat, "x")
    flat = scatter_sum(flat, "z")
    flat = gather_back(flat, "z")
    flat = gather_back(flat, "x")
    return flat.reshape(x.shape)


def chol_kernel(g_ref, out_ref):
    n = g_ref.shape[0]
    rows = lax.broadcasted_iota(jnp.int32, (n, n), 0)
    cols = lax.broadcasted_iota(jnp.int32, (n, n), 1)
    whole = jnp.concatenate([g_ref[...], jnp.where(rows == cols, 1.0, 0.0).astype(jnp.float32)], axis=1)
    lane_row = lax.broadcasted_iota(jnp.int32, (1, 2 * n), 1)
    for j in range(n):
        lo = j - j % 8
        if j % 8 == 0 and j > 0:
            out_ref[lo - 8 : lo, :] = whole[:8]
            whole = whole[8:]
        r = j - lo
        row = whole[r : r + 1]
        inverse = 1.0 / row[:, j : j + 1]
        kept = jnp.where(lane_row >= j, row, 0.0)
        top = kept * jnp.sqrt(inverse)
        sub = lax.broadcasted_iota(jnp.int32, whole.shape, 0)
        whole = jnp.where(
            sub > r, whole - whole[:, j : j + 1] * (kept * inverse), jnp.where(sub == r, top, whole)
        )
    out_ref[n - 8 :, :] = whole


def factor_block(g):
    n = g.shape[0]
    vmem = pl.BlockSpec(memory_space=pltpu.VMEM)
    out = pl.pallas_call(chol_kernel, out_shape=jax.ShapeDtypeStruct((n, 2 * n), jnp.float32),
        in_specs=[vmem], out_specs=vmem)(g)
    return out[:, :n].T, out[:, n:]


def shards(frames, tap_table, sketch_matrix, decay_rates):
    rows_here, frame_count = frames.shape
    npoints = rows_here * math.prod(lax.axis_size(a) for a in ROWS)
    batch_count = lax.axis_size(BATCH)
    coefs = (tap_table.astype(jnp.float32) / 1024.0).astype(jnp.bfloat16).astype(jnp.float32)
    inner, carry = band_blocks(coefs)
    nblocks = frame_count // BLOCK
    zero = jnp.zeros((BLOCK, BLOCK), jnp.bfloat16)
    main_band = jnp.block(
        [[inner if j == i else (carry if j == i + 1 else zero) for j in range(nblocks)] for i in range(nblocks)]
    )
    history = shifted(frames[:, frame_count - BLOCK :], BATCH, 1)
    main = jnp.dot(frames, main_band, preferred_element_type=jnp.float32)
    edge = jnp.dot(history, carry, preferred_element_type=jnp.float32)
    filtered = (main + jnp.pad(edge, ((0, 0), (0, frame_count - BLOCK)))).astype(jnp.bfloat16)
    factors = []
    factor = decay_rates[0]
    d = 1
    while d < batch_count:
        factors.append(factor)
        if 2 * d < batch_count:
            factor = factor * shifted(factor, BATCH, d)
        d *= 2
    sketch_matrix, factors = lax.optimization_barrier((sketch_matrix, factors))
    sketched = jnp.dot(filtered, sketch_matrix, preferred_element_type=jnp.float32)

    weighted = sketched
    d = 1
    for factor in factors:
        weighted = weighted + factor[None, :] * shifted(weighted, BATCH, d)
        d *= 2

    root_points = math.sqrt(npoints)
    rank_count = weighted.shape[1]
    both = jnp.concatenate([weighted, filtered.astype(jnp.float32)], axis=1)
    partial = lax.dot_general(
        weighted, both, (((0,), (0,)), ((), ())), precision=HIGH, preferred_element_type=jnp.float32
    )
    summed = reduce_rows(partial)
    gram = summed[:, :rank_count]
    cross = summed[:, rank_count:]
    lower_one, inverse = factor_block(gram)
    scaled = jnp.dot(weighted, inverse.T, precision=HIGH) * root_points
    projected = jnp.dot(inverse, cross, precision=HIGH) * (math.sqrt(rank_count) / root_points)
    upper = lower_one.T / root_points
    return (scaled[None], upper[None], projected[None])


def solution(mesh):
    rows_n, batch_n = mesh.devices.shape
    along_x = len({d.coords[0] for d in mesh.devices.flat})
    along_y = len({d.coords[1] for d in mesh.devices.flat})
    devices = mesh.devices.reshape(along_x, rows_n // along_x, along_y, batch_n // along_y)
    fine = Mesh(devices, ("x", "z", "y", "core"))
    placed = (P(ROWS, BATCH), P(), P(), P(BATCH, None))
    return jax.shard_map(
        shards,
        mesh=fine,
        in_specs=placed,
        out_specs=(P(BATCH, ROWS, None), P(BATCH, None, None), P(BATCH, None, None)),
        check_vma=False,
    )
```

```python
import math

import jax
import jax.numpy as jnp
from jax import lax
from jax.experimental import pallas as pl
from jax.experimental.pallas import tpu as pltpu
from jax.sharding import Mesh
from jax.sharding import PartitionSpec as P

HIGH = lax.Precision.HIGHEST
ROWS = ("x", "z")
BATCH = ("y", "core")
BLOCK = 128


def shifted(x, axis, by):
    length = lax.axis_size(axis)
    pairs = [(i, i + by) for i in range(length) if 0 <= i + by < length]
    return lax.ppermute(x, axis, pairs)


def band_kernel(coefs_ref, inner_ref, carry_ref):
    row_ids = lax.broadcasted_iota(jnp.int32, (BLOCK, BLOCK), 0)
    col_ids = lax.broadcasted_iota(jnp.int32, (BLOCK, BLOCK), 1)
    lag_ids = col_ids - row_ids
    inner = jnp.zeros((BLOCK, BLOCK), jnp.float32)
    carry = jnp.zeros((BLOCK, BLOCK), jnp.float32)
    for k in range(coefs_ref.shape[0]):
        tap = coefs_ref[k]
        inner = jnp.where(lag_ids == k, tap, inner)
        carry = jnp.where(lag_ids == k - BLOCK, tap, carry)
    inner_ref[...] = inner.astype(inner_ref.dtype)
    carry_ref[...] = carry.astype(carry_ref.dtype)


def band_blocks(coefs):
    block = jax.ShapeDtypeStruct((BLOCK, BLOCK), jnp.bfloat16)
    vmem = pl.BlockSpec(memory_space=pltpu.VMEM)
    return pl.pallas_call(
        band_kernel,
        out_shape=(block, block),
        in_specs=[pl.BlockSpec(memory_space=pltpu.SMEM)],
        out_specs=(vmem, vmem),
    )(coefs)


def scatter_sum(flat, axis):
    count = lax.axis_size(axis)
    got = lax.all_to_all(flat.reshape(count, -1), axis, 0, 0, tiled=True)
    return jnp.sum(got, axis=0)


def gather_back(flat, axis):
    count = lax.axis_size(axis)
    spread = jnp.broadcast_to(flat[None], (count,) + flat.shape)
    return lax.all_to_all(spread, axis, 0, 0, tiled=True).reshape(-1)


def reduce_rows(x):
    flat = x.reshape(-1)
    flat = scatter_sum(flat, "x")
    flat = scatter_sum(flat, "z")
    flat = gather_back(flat, "z")
    flat = gather_back(flat, "x")
    return flat.reshape(x.shape)


def chol_kernel(g_ref, out_ref):
    n = g_ref.shape[0]
    rows = lax.broadcasted_iota(jnp.int32, (n, n), 0)
    cols = lax.broadcasted_iota(jnp.int32, (n, n), 1)
    whole = jnp.concatenate([g_ref[...], jnp.where(rows == cols, 1.0, 0.0).astype(jnp.float32)], axis=1)
    lane_row = lax.broadcasted_iota(jnp.int32, (1, 2 * n), 1)
    for j in range(n):
        lo = j - j % 8
        if j % 8 == 0 and j > 0:
            out_ref[lo - 8 : lo, :] = whole[:8]
            whole = whole[8:]
        r = j - lo
        row = whole[r : r + 1]
        inverse = 1.0 / row[:, j : j + 1]
        kept = jnp.where(lane_row >= j, row, 0.0)
        top = kept * jnp.sqrt(inverse)
        sub = lax.broadcasted_iota(jnp.int32, whole.shape, 0)
        whole = jnp.where(
            sub > r, whole - whole[:, j : j + 1] * (kept * inverse), jnp.where(sub == r, top, whole)
        )
    out_ref[n - 8 :, :] = whole


def factor_block(g):
    n = g.shape[0]
    vmem = pl.BlockSpec(memory_space=pltpu.VMEM)
    out = pl.pallas_call(chol_kernel, out_shape=jax.ShapeDtypeStruct((n, 2 * n), jnp.float32),
        in_specs=[vmem], out_specs=vmem)(g)
    return out[:, :n].T, out[:, n:]


def shards(frames, tap_table, sketch_matrix, decay_rates):
    rows_here, frame_count = frames.shape
    npoints = rows_here * math.prod(lax.axis_size(a) for a in ROWS)
    batch_count = lax.axis_size(BATCH)
    coefs = (tap_table.astype(jnp.float32) / 1024.0).astype(jnp.bfloat16).astype(jnp.float32)
    inner, carry = band_blocks(coefs)
    nblocks = frame_count // BLOCK
    zero = jnp.zeros((BLOCK, BLOCK), jnp.bfloat16)
    band = jnp.block(
        [[carry if j == 0 else zero for j in range(nblocks)]]
        + [[inner if j == i else (carry if j == i + 1 else zero) for j in range(nblocks)] for i in range(nblocks)]
    )
    history = shifted(frames[:, frame_count - BLOCK :], BATCH, 1)
    extended = jnp.concatenate([history, frames], axis=1)
    filtered = jnp.dot(extended, band, preferred_element_type=jnp.float32).astype(jnp.bfloat16)
    sketched = jnp.dot(filtered, sketch_matrix, preferred_element_type=jnp.float32)

    factors = []
    factor = decay_rates[0]
    d = 1
    while d < batch_count:
        factors.append(factor)
        factor = factor * shifted(factor, BATCH, d)
        d *= 2
    weighted = sketched
    d = 1
    for factor in factors:
        weighted = weighted + factor[None, :] * shifted(weighted, BATCH, d)
        d *= 2

    root_points = math.sqrt(npoints)
    rank_count = weighted.shape[1]
    both = jnp.concatenate([weighted, filtered.astype(jnp.float32)], axis=1)
    partial = lax.dot_general(
        weighted, both, (((0,), (0,)), ((), ())), precision=HIGH, preferred_element_type=jnp.float32
    )
    summed = reduce_rows(partial)
    gram = summed[:, :rank_count]
    cross = summed[:, rank_count:]
    lower_one, inverse = factor_block(gram)
    scaled = jnp.dot(weighted, inverse.T, precision=HIGH) * root_points
    projected = jnp.dot(inverse, cross, precision=HIGH) * (math.sqrt(rank_count) / root_points)
    upper = lower_one.T / root_points
    return (scaled[None], upper[None], projected[None])


def solution(mesh):
    rows_n, batch_n = mesh.devices.shape
    along_x = len({d.coords[0] for d in mesh.devices.flat})
    along_y = len({d.coords[1] for d in mesh.devices.flat})
    devices = mesh.devices.reshape(along_x, rows_n // along_x, along_y, batch_n // along_y)
    fine = Mesh(devices, ("x", "z", "y", "core"))
    placed = (P(ROWS, BATCH), P(), P(), P(BATCH, None))
    return jax.shard_map(
        shards,
        mesh=fine,
        in_specs=placed,
        out_specs=(P(BATCH, ROWS, None), P(BATCH, None, None), P(BATCH, None, None)),
        check_vma=False,
    )
```
